256 devices in a mesh: tile: 64 (over x, z_lo, y), chan: 4 (over z_hi, core).
Axes of the slice: x: 4, y: 4, z: 8 (z_hi: 2, z_lo: 4; z = z_hi * 4 + z_lo), core: 2. Of those that a mesh axis runs over, the one named last changes fastest.
Arguments:
- latlon: bfloat16 [1, 16384, 8, 512], P(None, 'tile', None, 'chan'), may hold values from -6 to 6
- remap_weights: bfloat16 [64, 1156, 2048], P('tile'), may hold values from -0.1875 to 0.1875
- term_source: int32 [64, 256], replicated, may hold values from 0 to 63, as said below
- term_block: int32 [64, 256], replicated, may hold values from 0 to 255
- term_count: int32 [64], replicated, may hold values from 0 to 256, as said below
- rotation: int32 [64], P('tile'), may hold values from 0 to 3
- depthwise: bfloat16 [3, 3, 512], P(None, None, 'chan'), may hold values from -2 to 2
- pointwise: bfloat16 [512, 512], replicated, may hold values from -0.25 to 0.25
- cotangent: bfloat16 [1, 65536, 512], P(None, 'tile', 'chan'), may hold values from -6 to 6
Outputs:
- coupled: bfloat16 [1, 65536, 512], P(None, 'tile', 'chan')
- grad_latlon: bfloat16 [1, 16384, 8, 512], P(None, 'tile', None, 'chan')
- grad_depthwise: float32 [3, 3, 512], P(None, None, 'chan')
- grad_pointwise: float32 [512, 512], P('chan')
The draws below stay inside these ranges and needn't reach their ends.
Inputs may be any that keep to these rules, and one draw needn't show every extreme that they name: `term_source`: the first term_count[d] entries of row d name the source tile of each term and the rest are 0. Among the used entries of a row no source tile appears more than 6 times, and some row names a tile exactly 6 times. `term_count`: some face tile uses all 256 terms.
All inputs are finite; a program needn't handle non-finite values.
Results may differ from the reference program's by a relative error of at most 0.0059.
Values may be sent and summed in bfloat16 or wider, within the bound.
No kernel may reach another device: no remote copies, remote signals or barrier semaphores. Data moves between devices by JAX's collectives and lax.ppermute only.
A program may use at most 64 MiB of HBM per device.

```python
import jax
import jax.numpy as jnp
from jax import lax

CH = 512
TILE_EDGE = 32
SEG = 8
KMAX = 256
SRC_DEV = 256
BATCH = 1
CAP = 6
SOURCE_BLOCKS = 16384
EXT_CELLS = 1156
TERM_PTS = 2048
TILE_CELLS = 1024
TOTAL_CELLS = 65536
CELLS = 65536
N_TILE = 64


def term_tables(key):
    base_key = jax.random.fold_in(key, 4242)
    key_busy, key_forced, key_heavy, key_light = jax.random.split(base_key, 4)
    tile_ids = jnp.arange(N_TILE)
    busy_rows = jax.random.randint(key_busy, (N_TILE,), 0, 4) == 0
    forced = jax.random.randint(key_forced, (), 0, N_TILE)
    heavy_load = jax.random.randint(key_heavy, (N_TILE, N_TILE), CAP // 2, CAP + 1)
    light_load = jax.random.randint(key_light, (N_TILE, N_TILE), 0, CAP // 3 + 1)
    pair_count = jnp.where(busy_rows[:, None], heavy_load, light_load)
    pair_count = jnp.where((tile_ids == forced)[:, None], CAP, pair_count)
    before = jnp.cumsum(pair_count, axis=1) - pair_count
    pair_count = jnp.minimum(pair_count, jnp.maximum(KMAX - before, 0))
    through = jnp.cumsum(pair_count, axis=1)
    row_count = through[:, -1]
    positions = jnp.arange(KMAX)
    source = jnp.sum((through[:, None, :] <= positions[None, :, None]).astype(jnp.int32), axis=2)
    source = jnp.where(positions[None, :] < row_count[:, None], source, 0)
    return (source.astype(jnp.int32), row_count.astype(jnp.int32))


def draw_term_source(key, part):
    return term_tables(key)[0]


def draw_term_count(key, part):
    return term_tables(key)[1]


def with_ends(entries, own_key, least, high):
    longest = entries.shape.index(max(entries.shape))
    spots = []
    for shift in (0, 1):
        where = [jax.random.randint(jax.random.fold_in(own_key, axis), (), 0, length) for axis, length in enumerate(entries.shape)]
        where[longest] = (where[longest] + shift) % entries.shape[longest]
        spots.append(tuple(where))
    return entries.at[spots[0]].set(least).at[spots[1]].set(high)


def block_scale(rng, shape, cuts, low, largest):
    loudness, own = 1.0, jax.random.fold_in(rng, 6)
    for axis_at, shards_of in cuts:
        heights = jnp.exp(jax.random.uniform(jax.random.fold_in(own, axis_at), (shards_of,), jnp.float32, low / len(cuts), largest / len(cuts)))
        loudness = loudness * jnp.repeat(heights, shape[axis_at] // shards_of).reshape([-1 if axis == axis_at else 1 for axis in range(len(shape))])
    return loudness


def gaussian(own_key, extent, width, most, cuts=(), kind=jnp.bfloat16):
    result = width * jax.random.normal(own_key, extent, jnp.float32)
    if cuts:
        result = result * block_scale(own_key, extent, cuts, -0.22, 0.18)
    return jnp.clip(result, -most, most).astype(kind)


def setup_inputs(seed: int = 0) -> dict:
    keys = jax.random.split(jax.random.key(seed), 10)
    latlon = gaussian(keys[0], (BATCH, SOURCE_BLOCKS, SEG, CH), 1.0, 6.0, ((1, 64), (3, 4)))
    remap_weights = gaussian(keys[1], (N_TILE, EXT_CELLS, TERM_PTS), (TERM_PTS // 2) ** -0.5, 0.1875, ((0, 64),))
    term_source = draw_term_source(jax.random.fold_in(keys[9], 71), 0)
    term_block = with_ends(jax.random.randint(keys[3], (N_TILE, KMAX), 0, SRC_DEV), jax.random.fold_in(keys[3], 1), 0, SRC_DEV - 1).astype(jnp.int32)
    term_count = draw_term_count(jax.random.fold_in(keys[9], 71), 0)
    rotation = with_ends(jax.random.randint(keys[5], (N_TILE,), 0, 4), jax.random.fold_in(keys[5], 1), 0, 3).astype(jnp.int32)
    depthwise = gaussian(keys[6], (3, 3, CH), 9 ** -0.5, 2.0, ((2, 4),))
    pointwise = gaussian(keys[7], (CH, CH), CH ** -0.5, 0.25)
    cotangent = gaussian(keys[8], (BATCH, TOTAL_CELLS, CH), 1.0, 6.0, ((1, 64), (2, 4)))
    return dict(latlon=latlon, remap_weights=remap_weights, term_source=term_source, term_block=term_block, term_count=term_count, rotation=rotation, depthwise=depthwise, pointwise=pointwise, cotangent=cotangent)


def turn_kernel(kernel, turn, direction):
    turned = jnp.zeros_like(kernel)
    for quarter in range(4):
        turned = turned + jnp.where(turn == quarter, jnp.rot90(kernel, direction * quarter, axes=(0, 1)), 0.0)
    return turned


def stencil_apply(field, kernel):
    shape_out = (field.shape[0], TILE_EDGE, TILE_EDGE, field.shape[3])
    hidden = jnp.zeros(shape_out, jnp.float32)
    for row_off in range(3):
        for col_off in range(3):
            window = field[:, row_off:row_off + TILE_EDGE, col_off:col_off + TILE_EDGE, :].astype(jnp.float32)
            hidden = hidden + kernel[row_off, col_off] * window
    return hidden


def stencil_grads(field, kernel, grad_hidden):
    tap_rows = []
    grad_field = jnp.zeros(field.shape, jnp.float32)
    for row_off in range(3):
        tap_cols = []
        for col_off in range(3):
            window = field[:, row_off:row_off + TILE_EDGE, col_off:col_off + TILE_EDGE, :].astype(jnp.float32)
            tap_cols.append(jnp.sum(window * grad_hidden, axis=(0, 1, 2)))
            spread = kernel[row_off, col_off] * grad_hidden
            grad_field = grad_field + jnp.pad(spread, ((0, 0), (row_off, 2 - row_off), (col_off, 2 - col_off), (0, 0)))
        tap_rows.append(jnp.stack(tap_cols))
    return jnp.stack(tap_rows), grad_field


def reference(latlon, remap_weights, term_source, term_block, term_count, rotation, depthwise, pointwise, cotangent):
    kernel = depthwise.astype(jnp.float32)
    positions = jnp.arange(KMAX, dtype=jnp.int32)

    def one_tile(carry, tile_id):
        kernel_sum, mix_sum = carry
        in_use = positions < term_count[tile_id]
        block_index = (term_source[tile_id] * SRC_DEV + term_block[tile_id]).astype(jnp.int32)
        gathered = jnp.take(latlon, block_index, axis=1)
        gathered = jnp.where(in_use[None, :, None, None], gathered, jnp.zeros((), latlon.dtype))
        gathered = gathered.reshape(BATCH, TERM_PTS, CH)
        weights = remap_weights[tile_id].astype(jnp.float32)
        remapped = jnp.einsum("pk,bkc->bpc", weights, gathered.astype(jnp.float32)).astype(jnp.bfloat16)
        field = remapped.reshape(BATCH, TILE_EDGE + 2, TILE_EDGE + 2, CH)
        turned = turn_kernel(kernel, rotation[tile_id], 1)
        hidden = stencil_apply(field, turned)
        active = jax.nn.silu(hidden).astype(jnp.bfloat16).reshape(BATCH * TILE_CELLS, CH)
        mixed = jnp.dot(active, pointwise, preferred_element_type=jnp.float32).astype(jnp.bfloat16)
        upstream = lax.dynamic_slice_in_dim(cotangent, tile_id * TILE_CELLS, TILE_CELLS, 1)
        upstream = upstream.reshape(BATCH * TILE_CELLS, CH)
        grad_active = jnp.dot(upstream, pointwise.T, preferred_element_type=jnp.float32)
        sigma = jax.nn.sigmoid(hidden)
        grad_hidden = grad_active.reshape(hidden.shape) * sigma * (1.0 + hidden * (1.0 - sigma))
        grad_mix = jnp.dot(active.T, upstream, preferred_element_type=jnp.float32)
        grad_turned, grad_field = stencil_grads(field, turned, grad_hidden)
        grad_kernel = turn_kernel(grad_turned, rotation[tile_id], -1)
        grad_field = grad_field.astype(jnp.bfloat16).reshape(BATCH, EXT_CELLS, CH)
        grad_terms = jnp.einsum("pk,bpc->bkc", weights, grad_field.astype(jnp.float32))
        grad_terms = grad_terms.reshape(BATCH, KMAX, SEG, CH)
        grad_terms = jnp.where(in_use[None, :, None, None], grad_terms, 0.0).astype(jnp.bfloat16)
        outputs = (mixed.reshape(BATCH, TILE_CELLS, CH), grad_terms, block_index)
        return (kernel_sum + grad_kernel, mix_sum + grad_mix), outputs

    start_carry = (jnp.zeros((3, 3, CH), jnp.float32), jnp.zeros((CH, CH), jnp.float32))
    sums, stacked = lax.scan(one_tile, start_carry, jnp.arange(N_TILE, dtype=jnp.int32))
    kernel_sum, mix_sum = sums
    mixed_all, terms_all, blocks_all = stacked
    coupled = jnp.transpose(mixed_all, (1, 0, 2, 3)).reshape(BATCH, TOTAL_CELLS, CH)
    terms_flat = jnp.transpose(terms_all, (1, 0, 2, 3, 4)).reshape(BATCH, N_TILE * KMAX, SEG, CH)
    grad_latlon = jnp.zeros((BATCH, SOURCE_BLOCKS, SEG, CH), jnp.float32)
    grad_latlon = grad_latlon.at[:, blocks_all.reshape(-1)].add(terms_flat.astype(jnp.float32))
    factor = 1.0 / (CELLS ** 0.5)
    return coupled, grad_latlon.astype(jnp.bfloat16), kernel_sum * factor, mix_sum * factor
```

```python
import math

import jax
import jax.numpy as jnp
from jax import lax
from jax.sharding import Mesh, PartitionSpec as P

TILE_EDGE = 32
TILE = ("x", "zl", "y")
CHAN = ("zh", "core")


def turn_kernel(kernel, turn, direction):
    turned = jnp.zeros_like(kernel)
    for quarter in range(4):
        turned = turned + jnp.where(
            turn == quarter, jnp.rot90(kernel, direction * quarter, axes=(0, 1)), 0.0
        )
    return turned


def stencil_apply(field, kernel):
    shape_out = (field.shape[0], TILE_EDGE, TILE_EDGE, field.shape[3])
    hidden = jnp.zeros(shape_out, jnp.float32)
    for row_off in range(3):
        for col_off in range(3):
            window = field[
                :, row_off : row_off + TILE_EDGE, col_off : col_off + TILE_EDGE, :
            ].astype(jnp.float32)
            hidden = hidden + kernel[row_off, col_off] * window
    return hidden


def stencil_grads(field, kernel, grad_hidden):
    tap_rows = []
    grad_field = jnp.zeros(field.shape, jnp.float32)
    for row_off in range(3):
        tap_cols = []
        for col_off in range(3):
            window = field[
                :, row_off : row_off + TILE_EDGE, col_off : col_off + TILE_EDGE, :
            ].astype(jnp.float32)
            tap_cols.append(jnp.sum(window * grad_hidden, axis=(0, 1, 2)))
            spread = kernel[row_off, col_off] * grad_hidden
            grad_field = grad_field + jnp.pad(
                spread, ((0, 0), (row_off, 2 - row_off), (col_off, 2 - col_off), (0, 0))
            )
        tap_rows.append(jnp.stack(tap_cols))
    return (jnp.stack(tap_rows), grad_field)


def body(
    latlon,
    remap_weights,
    term_source,
    term_block,
    term_count,
    rotation,
    depthwise,
    pointwise,
    cotangent,
):
    tile_now = lax.axis_index(TILE)
    tile_total = term_source.shape[0]
    chan_now = lax.axis_index(CHAN)
    batch_rows, block_total, seg_len, chan_local = latlon.shape
    terms_max = term_source.shape[1]
    capacity = 3 * terms_max // (2 * tile_total)
    ext_edge = TILE_EDGE + 2
    tile_cells = TILE_EDGE * TILE_EDGE
    flat_rows = batch_rows * tile_cells
    positions = jnp.arange(terms_max, dtype=jnp.int32)
    in_use = positions[None, :] < term_count[:, None]
    mine = in_use & (term_source == tile_now)
    send_rank = jnp.cumsum(mine.astype(jnp.int32), axis=1) - 1
    slot_ids = jnp.arange(capacity, dtype=jnp.int32)
    slot_hits = mine[:, :, None] & (send_rank[:, :, None] == slot_ids[None, None, :])
    slot_filled = jnp.any(slot_hits, axis=1).reshape(-1)
    slot_block = jnp.sum(jnp.where(slot_hits, term_block[:, :, None], 0), axis=1).reshape(-1)
    outgoing = jnp.take(latlon, slot_block, axis=1)
    outgoing = jnp.where(slot_filled[None, :, None, None], outgoing, jnp.zeros((), latlon.dtype))
    own_source = lax.dynamic_index_in_dim(term_source, tile_now, 0, keepdims=False)
    own_count = lax.dynamic_index_in_dim(term_count, tile_now, 0, keepdims=False)
    own_use = positions < own_count
    same_source = (
        (own_source[None, :] == own_source[:, None])
        & own_use[None, :]
        & (positions[None, :] <= positions[:, None])
    )
    own_rank = jnp.sum(same_source.astype(jnp.int32), axis=1) - 1
    recv_slot = jnp.where(own_use, own_source * capacity + own_rank, 0)
    return_slot = jnp.where(own_use, own_source * capacity + own_rank, tile_total * capacity)
    weights = remap_weights[0]
    ext_cells = weights.shape[0]
    term_pts = weights.shape[1]
    arrived = lax.all_to_all(outgoing, TILE, split_axis=1, concat_axis=1, tiled=True)
    picked = jnp.take(arrived, recv_slot, axis=1)
    picked = jnp.where(own_use[None, :, None, None], picked, jnp.zeros((), arrived.dtype))
    picked = picked.reshape(picked.shape[0], term_pts, chan_local)
    mapped = jnp.einsum("pk,bkc->bpc", weights, picked, preferred_element_type=jnp.float32)
    remapped = mapped.astype(jnp.bfloat16)
    field = remapped.reshape(batch_rows, ext_edge, ext_edge, chan_local)
    turn = rotation[0]
    kernel = turn_kernel(depthwise.astype(jnp.float32), turn, 1)
    hidden = stencil_apply(field, kernel)
    active = jax.nn.silu(hidden).astype(jnp.bfloat16).reshape(flat_rows, chan_local)
    own_rows = lax.dynamic_slice_in_dim(pointwise, chan_now * chan_local, chan_local, 0)
    own_cols = lax.dynamic_slice_in_dim(pointwise, chan_now * chan_local, chan_local, 1)
    active_all = lax.all_gather(active, CHAN, axis=1, tiled=True)
    mixed = jnp.dot(active_all, own_cols, preferred_element_type=jnp.float32)
    coupled = mixed.astype(jnp.bfloat16).reshape(batch_rows, tile_cells, chan_local)
    upstream = cotangent.reshape(flat_rows, chan_local)
    piece = lax.all_gather(upstream, CHAN, axis=1, tiled=True)
    grad_active = lax.dot_general(
        piece, own_rows, (((1,), (1,)), ((), ())), preferred_element_type=jnp.float32
    )
    block_grad = lax.dot_general(
        active, piece, (((0,), (0,)), ((), ())), preferred_element_type=jnp.float32
    )
    grad_mix = block_grad
    grad_active, grad_mix = (grad_active, grad_mix)
    sigma = jax.nn.sigmoid(hidden)
    grad_hidden = grad_active.reshape(hidden.shape) * sigma * (1.0 + hidden * (1.0 - sigma))
    grad_turned, grad_field = stencil_grads(field, kernel, grad_hidden)
    grad_field = grad_field.astype(jnp.bfloat16).reshape(batch_rows, ext_cells, chan_local)
    grad_terms = jnp.einsum("pk,bpc->bkc", weights, grad_field, preferred_element_type=jnp.float32)
    grad_terms = grad_terms.reshape(batch_rows, terms_max, seg_len, chan_local)
    grad_terms = jnp.where(own_use[None, :, None, None], grad_terms, 0.0).astype(jnp.bfloat16)
    returning = jnp.zeros((batch_rows, tile_total * capacity, seg_len, chan_local), jnp.bfloat16)
    returning = returning.at[:, return_slot].set(grad_terms, mode="drop")
    landing = jnp.where(slot_filled, slot_block, block_total)
    arrived = lax.all_to_all(returning, TILE, split_axis=1, concat_axis=1, tiled=True)
    summed = jnp.zeros((arrived.shape[0], block_total, seg_len, chan_local), jnp.float32)
    summed = summed.at[:, landing].add(arrived.astype(jnp.float32), mode="drop")
    grad_latlon = summed.astype(jnp.bfloat16)
    grad_kernel = turn_kernel(grad_turned, turn, -1)
    packed = jnp.concatenate([grad_kernel.reshape(-1), grad_mix.reshape(-1)])
    for axis in TILE:
        packed = lax.psum(packed, axis)
    kernel_sum = packed[: grad_kernel.size].reshape(grad_kernel.shape)
    mix_sum = packed[grad_kernel.size :].reshape(grad_mix.shape)
    factor = 1.0 / math.sqrt(batch_rows * tile_cells * tile_total)
    return (coupled, grad_latlon, kernel_sum * factor, mix_sum * factor)


def physical_mesh(mesh):
    devices = mesh.devices
    tile_devs = devices[:, 0]
    x_count = len({d.coords[0] for d in tile_devs})
    y_count = len({d.coords[1] for d in tile_devs})
    zl_count = tile_devs.size // (x_count * y_count)
    zh_count = len({d.coords[2] for d in devices[0, :]})
    core_count = devices.shape[1] // zh_count
    shaped = devices.reshape(x_count, zl_count, y_count, zh_count, core_count)
    return Mesh(shaped, TILE + CHAN)


def solution(mesh):
    mesh = physical_mesh(mesh)
    return jax.shard_map(
        body,
        mesh=mesh,
        in_specs=(
            P(None, TILE, None, CHAN),
            P(TILE, None, None),
            P(),
            P(),
            P(),
            P(TILE),
            P(None, None, CHAN),
            P(),
            P(None, TILE, CHAN),
        ),
        out_specs=(
            P(None, TILE, CHAN),
            P(None, TILE, None, CHAN),
            P(None, None, CHAN),
            P(CHAN, None),
        ),
        check_vma=False,
    )
```

```python
import math

import jax
import jax.numpy as jnp
from jax import lax
from jax.sharding import Mesh, PartitionSpec as P

TILE_EDGE = 32
TILE = ("x", "zl", "y")
CHAN = ("zh", "core")


def turn_kernel(kernel, turn, direction):
    turned = jnp.zeros_like(kernel)
    for quarter in range(4):
        turned = turned + jnp.where(
            turn == quarter, jnp.rot90(kernel, direction * quarter, axes=(0, 1)), 0.0
        )
    return turned


def stencil_apply(field, kernel):
    shape_out = (field.shape[0], TILE_EDGE, TILE_EDGE, field.shape[3])
    hidden = jnp.zeros(shape_out, jnp.float32)
    for row_off in range(3):
        for col_off in range(3):
            window = field[
                :, row_off : row_off + TILE_EDGE, col_off : col_off + TILE_EDGE, :
            ].astype(jnp.float32)
            hidden = hidden + kernel[row_off, col_off] * window
    return hidden


def stencil_grads(field, kernel, grad_hidden):
    tap_rows = []
    grad_field = jnp.zeros(field.shape, jnp.float32)
    for row_off in range(3):
        tap_cols = []
        for col_off in range(3):
            window = field[
                :, row_off : row_off + TILE_EDGE, col_off : col_off + TILE_EDGE, :
            ].astype(jnp.float32)
            tap_cols.append(jnp.sum(window * grad_hidden, axis=(0, 1, 2)))
            spread = kernel[row_off, col_off] * grad_hidden
            grad_field = grad_field + jnp.pad(
                spread, ((0, 0), (row_off, 2 - row_off), (col_off, 2 - col_off), (0, 0))
            )
        tap_rows.append(jnp.stack(tap_cols))
    return (jnp.stack(tap_rows), grad_field)


def tile_sum(flat, parts):
    total = flat.shape[0]
    width = -(-total // (parts * 128)) * 128
    rows = jnp.pad(flat, (0, parts * width - total)).reshape(parts, width)
    pieces = lax.all_to_all(rows, TILE, split_axis=0, concat_axis=0, tiled=True)
    mine = jnp.sum(pieces, axis=0)
    spread = jnp.broadcast_to(mine[None, :], (parts, width))
    whole = lax.all_to_all(spread, TILE, split_axis=0, concat_axis=0, tiled=True)
    return whole.reshape(-1)[:total]


def body(
    latlon,
    remap_weights,
    term_source,
    term_block,
    term_count,
    rotation,
    depthwise,
    pointwise,
    cotangent,
):
    tile_now = lax.axis_index(TILE)
    tile_total = term_source.shape[0]
    chan_now = lax.axis_index(CHAN)
    batch_rows, block_total, seg_len, chan_local = latlon.shape
    terms_max = term_source.shape[1]
    capacity = 3 * terms_max // (2 * tile_total)
    ext_edge = TILE_EDGE + 2
    tile_cells = TILE_EDGE * TILE_EDGE
    flat_rows = batch_rows * tile_cells
    positions = jnp.arange(terms_max, dtype=jnp.int32)
    in_use = positions[None, :] < term_count[:, None]
    mine = in_use & (term_source == tile_now)
    send_rank = jnp.cumsum(mine.astype(jnp.int32), axis=1) - 1
    slot_ids = jnp.arange(capacity, dtype=jnp.int32)
    slot_hits = mine[:, :, None] & (send_rank[:, :, None] == slot_ids[None, None, :])
    slot_filled = jnp.any(slot_hits, axis=1).reshape(-1)
    slot_block = jnp.sum(jnp.where(slot_hits, term_block[:, :, None], 0), axis=1).reshape(-1)
    outgoing = jnp.take(latlon, slot_block, axis=1)
    outgoing = jnp.where(slot_filled[None, :, None, None], outgoing, jnp.zeros((), latlon.dtype))
    own_source = lax.dynamic_index_in_dim(term_source, tile_now, 0, keepdims=False)
    own_count = lax.dynamic_index_in_dim(term_count, tile_now, 0, keepdims=False)
    own_use = positions < own_count
    same_source = (
        (own_source[None, :] == own_source[:, None])
        & own_use[None, :]
        & (positions[None, :] <= positions[:, None])
    )
    own_rank = jnp.sum(same_source.astype(jnp.int32), axis=1) - 1
    recv_slot = jnp.where(own_use, own_source * capacity + own_rank, 0)
    return_slot = jnp.where(own_use, own_source * capacity + own_rank, tile_total * capacity)
    weights = remap_weights[0]
    ext_cells = weights.shape[0]
    term_pts = weights.shape[1]
    arrived = lax.all_to_all(outgoing, TILE, split_axis=1, concat_axis=1, tiled=True)
    picked = jnp.take(arrived, recv_slot, axis=1)
    picked = jnp.where(own_use[None, :, None, None], picked, jnp.zeros((), arrived.dtype))
    picked = picked.reshape(picked.shape[0], term_pts, chan_local)
    mapped = jnp.einsum("pk,bkc->bpc", weights, picked, preferred_element_type=jnp.float32)
    remapped = mapped.astype(jnp.bfloat16)
    field = remapped.reshape(batch_rows, ext_edge, ext_edge, chan_local)
    turn = rotation[0]
    kernel = turn_kernel(depthwise.astype(jnp.float32), turn, 1)
    hidden = stencil_apply(field, kernel)
    active = jax.nn.silu(hidden).astype(jnp.bfloat16).reshape(flat_rows, chan_local)
    own_rows = lax.dynamic_slice_in_dim(pointwise, chan_now * chan_local, chan_local, 0)
    own_cols = lax.dynamic_slice_in_dim(pointwise, chan_now * chan_local, chan_local, 1)
    active_all = lax.all_gather(active, CHAN, axis=1, tiled=True)
    mixed = jnp.dot(active_all, own_cols, preferred_element_type=jnp.float32)
    coupled = mixed.astype(jnp.bfloat16).reshape(batch_rows, tile_cells, chan_local)
    upstream = cotangent.reshape(flat_rows, chan_local)
    piece = lax.all_gather(upstream, CHAN, axis=1, tiled=True)
    grad_active = lax.dot_general(
        piece, own_rows, (((1,), (1,)), ((), ())), preferred_element_type=jnp.float32
    )
    block_grad = lax.dot_general(
        active, piece, (((0,), (0,)), ((), ())), preferred_element_type=jnp.float32
    )
    grad_mix = block_grad
    grad_active, grad_mix = (grad_active, grad_mix)
    sigma = jax.nn.sigmoid(hidden)
    grad_hidden = grad_active.reshape(hidden.shape) * sigma * (1.0 + hidden * (1.0 - sigma))
    grad_turned, grad_field = stencil_grads(field, kernel, grad_hidden)
    grad_field = grad_field.astype(jnp.bfloat16).reshape(batch_rows, ext_cells, chan_local)
    grad_terms = jnp.einsum("pk,bpc->bkc", weights, grad_field, preferred_element_type=jnp.float32)
    grad_terms = grad_terms.reshape(batch_rows, terms_max, seg_len, chan_local)
    grad_terms = jnp.where(own_use[None, :, None, None], grad_terms, 0.0).astype(jnp.bfloat16)
    slot_all = jnp.arange(tile_total * capacity, dtype=jnp.int32)
    place = (slot_all[:, None] == return_slot[None, :]).astype(jnp.bfloat16)
    returning = jnp.einsum(
        "st,btc->bsc", place, grad_terms.reshape(batch_rows, terms_max, seg_len * chan_local),
        preferred_element_type=jnp.float32,
    ).astype(jnp.bfloat16).reshape(batch_rows, tile_total * capacity, seg_len, chan_local)
    landing = jnp.where(slot_filled, slot_block, block_total)
    arrived = lax.all_to_all(returning, TILE, split_axis=1, concat_axis=1, tiled=True)
    block_ids = jnp.arange(block_total, dtype=jnp.int32)
    gather_back = (block_ids[:, None] == landing[None, :]).astype(jnp.bfloat16)
    summed = jnp.einsum(
        "ks,bsc->bkc", gather_back, arrived.reshape(batch_rows, tile_total * capacity, seg_len * chan_local),
        preferred_element_type=jnp.float32,
    )
    grad_latlon = summed.astype(jnp.bfloat16).reshape(batch_rows, block_total, seg_len, chan_local)
    grad_kernel = turn_kernel(grad_turned, turn, -1)
    packed = jnp.concatenate([grad_kernel.reshape(-1), grad_mix.reshape(-1)])
    packed = tile_sum(packed, tile_total)
    kernel_sum = packed[: grad_kernel.size].reshape(grad_kernel.shape)
    mix_sum = packed[grad_kernel.size :].reshape(grad_mix.shape)
    factor = 1.0 / math.sqrt(batch_rows * tile_cells * tile_total)
    return (coupled, grad_latlon, kernel_sum * factor, mix_sum * factor)


def physical_mesh(mesh):
    devices = mesh.devices
    tile_devs = devices[:, 0]
    x_count = len({d.coords[0] for d in tile_devs})
    y_count = len({d.coords[1] for d in tile_devs})
    zl_count = tile_devs.size // (x_count * y_count)
    zh_count = len({d.coords[2] for d in devices[0, :]})
    core_count = devices.shape[1] // zh_count
    shaped = devices.reshape(x_count, zl_count, y_count, zh_count, core_count)
    return Mesh(shaped, TILE + CHAN)


def solution(mesh):
    mesh = physical_mesh(mesh)
    return jax.shard_map(
        body,
        mesh=mesh,
        in_specs=(
            P(None, TILE, None, CHAN),
            P(TILE, None, None),
            P(),
            P(),
            P(),
            P(TILE),
            P(None, None, CHAN),
            P(),
            P(None, TILE, CHAN),
        ),
        out_specs=(
            P(None, TILE, CHAN),
            P(None, TILE, None, CHAN),
            P(None, None, CHAN),
            P(CHAN, None),
        ),
        check_vma=False,
    )
```

```python
import math

import jax
import jax.numpy as jnp
from jax import lax
from jax.sharding import Mesh, PartitionSpec as P

TILE_EDGE = 32
TILE = ("x", "zl", "y")
CHAN = ("zh", "core")


def turn_kernel(kernel, turn, direction):
    turned = jnp.zeros_like(kernel)
    for quarter in range(4):
        turned = turned + jnp.where(
            turn == quarter, jnp.rot90(kernel, direction * quarter, axes=(0, 1)), 0.0
        )
    return turned


def stencil_apply(field, kernel):
    shape_out = (field.shape[0], TILE_EDGE, TILE_EDGE, field.shape[3])
    hidden = jnp.zeros(shape_out, jnp.float32)
    for row_off in range(3):
        for col_off in range(3):
            window = field[
                :, row_off : row_off + TILE_EDGE, col_off : col_off + TILE_EDGE, :
            ].astype(jnp.float32)
            hidden = hidden + kernel[row_off, col_off] * window
    return hidden


def stencil_grads(field, kernel, grad_hidden):
    tap_rows = []
    grad_field = jnp.zeros(field.shape, jnp.float32)
    for row_off in range(3):
        tap_cols = []
        for col_off in range(3):
            window = field[
                :, row_off : row_off + TILE_EDGE, col_off : col_off + TILE_EDGE, :
            ].astype(jnp.float32)
            tap_cols.append(jnp.sum(window * grad_hidden, axis=(0, 1, 2)))
            spread = kernel[row_off, col_off] * grad_hidden
            grad_field = grad_field + jnp.pad(
                spread, ((0, 0), (row_off, 2 - row_off), (col_off, 2 - col_off), (0, 0))
            )
        tap_rows.append(jnp.stack(tap_cols))
    return (jnp.stack(tap_rows), grad_field)


def tile_partial(flat, parts):
    total = flat.shape[0]
    width = -(-total // (parts * 128)) * 128
    rows = jnp.pad(flat, (0, parts * width - total)).reshape(parts, width)
    pieces = lax.all_to_all(rows, TILE, split_axis=0, concat_axis=0, tiled=True)
    return jnp.sum(pieces, axis=0)


def as_word_pair(value):
    high = lax.reduce_precision(value, exponent_bits=8, mantissa_bits=7)
    low = value - high
    return jnp.concatenate([high.astype(jnp.bfloat16), low.astype(jnp.bfloat16)])


def from_word_pair(words):
    width = words.shape[-1] // 2
    return words[..., :width].astype(jnp.float32) + words[..., width:].astype(jnp.float32)


def body(
    latlon,
    remap_weights,
    term_source,
    term_block,
    term_count,
    rotation,
    depthwise,
    pointwise,
    cotangent,
):
    tile_now = lax.axis_index(TILE)
    tile_total = term_source.shape[0]
    chan_now = lax.axis_index(CHAN)
    batch_rows, block_total, seg_len, chan_local = latlon.shape
    terms_max = term_source.shape[1]
    capacity = 3 * terms_max // (2 * tile_total)
    ext_edge = TILE_EDGE + 2
    tile_cells = TILE_EDGE * TILE_EDGE
    flat_rows = batch_rows * tile_cells
    positions = jnp.arange(terms_max, dtype=jnp.int32)
    in_use = positions[None, :] < term_count[:, None]
    mine = in_use & (term_source == tile_now)
    send_rank = jnp.cumsum(mine.astype(jnp.int32), axis=1) - 1
    slot_ids = jnp.arange(capacity, dtype=jnp.int32)
    slot_hits = mine[:, :, None] & (send_rank[:, :, None] == slot_ids[None, None, :])
    slot_filled = jnp.any(slot_hits, axis=1).reshape(-1)
    slot_block = jnp.sum(jnp.where(slot_hits, term_block[:, :, None], 0), axis=1).reshape(-1)
    outgoing = jnp.take(latlon, slot_block, axis=1)
    outgoing = jnp.where(slot_filled[None, :, None, None], outgoing, jnp.zeros((), latlon.dtype))
    own_source = lax.dynamic_index_in_dim(term_source, tile_now, 0, keepdims=False)
    own_count = lax.dynamic_index_in_dim(term_count, tile_now, 0, keepdims=False)
    own_use = positions < own_count
    same_source = (
        (own_source[None, :] == own_source[:, None])
        & own_use[None, :]
        & (positions[None, :] <= positions[:, None])
    )
    own_rank = jnp.sum(same_source.astype(jnp.int32), axis=1) - 1
    recv_slot = jnp.where(own_use, own_source * capacity + own_rank, 0)
    return_slot = jnp.where(own_use, own_source * capacity + own_rank, tile_total * capacity)
    weights = remap_weights[0]
    ext_cells = weights.shape[0]
    term_pts = weights.shape[1]
    arrived = lax.all_to_all(outgoing, TILE, split_axis=1, concat_axis=1, tiled=True)
    picked = jnp.take(arrived, recv_slot, axis=1)
    picked = jnp.where(own_use[None, :, None, None], picked, jnp.zeros((), arrived.dtype))
    picked = picked.reshape(picked.shape[0], term_pts, chan_local)
    mapped = jnp.einsum("pk,bkc->bpc", weights, picked, preferred_element_type=jnp.float32)
    remapped = mapped.astype(jnp.bfloat16)
    field = remapped.reshape(batch_rows, ext_edge, ext_edge, chan_local)
    turn = rotation[0]
    kernel = turn_kernel(depthwise.astype(jnp.float32), turn, 1)
    hidden = stencil_apply(field, kernel)
    active = jax.nn.silu(hidden).astype(jnp.bfloat16).reshape(flat_rows, chan_local)
    own_rows = lax.dynamic_slice_in_dim(pointwise, chan_now * chan_local, chan_local, 0)
    own_cols = lax.dynamic_slice_in_dim(pointwise, chan_now * chan_local, chan_local, 1)
    active_all = lax.all_gather(active, CHAN, axis=1, tiled=True)
    mixed = jnp.dot(active_all, own_cols, preferred_element_type=jnp.float32)
    coupled = mixed.astype(jnp.bfloat16).reshape(batch_rows, tile_cells, chan_local)
    upstream = cotangent.reshape(flat_rows, chan_local)
    piece = lax.all_gather(upstream, CHAN, axis=1, tiled=True)
    grad_active = lax.dot_general(
        piece, own_rows, (((1,), (1,)), ((), ())), preferred_element_type=jnp.float32
    )
    block_grad = lax.dot_general(
        active, piece, (((0,), (0,)), ((), ())), preferred_element_type=jnp.float32
    )
    grad_mix = block_grad
    grad_active, grad_mix = (grad_active, grad_mix)
    sigma = jax.nn.sigmoid(hidden)
    grad_hidden = grad_active.reshape(hidden.shape) * sigma * (1.0 + hidden * (1.0 - sigma))
    grad_turned, grad_field = stencil_grads(field, kernel, grad_hidden)
    grad_field = grad_field.astype(jnp.bfloat16).reshape(batch_rows, ext_cells, chan_local)
    grad_terms = jnp.einsum("pk,bpc->bkc", weights, grad_field, preferred_element_type=jnp.float32)
    grad_terms = grad_terms.reshape(batch_rows, terms_max, seg_len, chan_local)
    grad_terms = jnp.where(own_use[None, :, None, None], grad_terms, 0.0).astype(jnp.bfloat16)
    slot_all = jnp.arange(tile_total * capacity, dtype=jnp.int32)
    place = (slot_all[:, None] == return_slot[None, :]).astype(jnp.bfloat16)
    returning = jnp.einsum(
        "st,btc->bsc", place, grad_terms.reshape(batch_rows, terms_max, seg_len * chan_local),
        preferred_element_type=jnp.float32,
    ).astype(jnp.bfloat16).reshape(batch_rows, tile_total * capacity, seg_len, chan_local)
    landing = jnp.where(slot_filled, slot_block, block_total)
    grad_kernel = turn_kernel(grad_turned, turn, -1)
    packed = jnp.concatenate([grad_kernel.reshape(-1), grad_mix.reshape(-1)])
    my_slot = tile_partial(packed, tile_total)
    slot_words = as_word_pair(my_slot)
    block_width = capacity * seg_len * chan_local
    payload = jnp.concatenate(
        [
            returning.reshape(tile_total, block_width),
            jnp.broadcast_to(slot_words[None, :], (tile_total, slot_words.shape[0])),
        ],
        axis=1,
    )
    arrived_all = lax.all_to_all(payload, TILE, split_axis=0, concat_axis=0, tiled=True)
    arrived = arrived_all[:, :block_width].reshape(batch_rows, tile_total * capacity, seg_len, chan_local)
    packed = from_word_pair(arrived_all[:, block_width:]).reshape(-1)[: packed.shape[0]]
    block_ids = jnp.arange(block_total, dtype=jnp.int32)
    gather_back = (block_ids[:, None] == landing[None, :]).astype(jnp.bfloat16)
    summed = jnp.einsum(
        "ks,bsc->bkc", gather_back, arrived.reshape(batch_rows, tile_total * capacity, seg_len * chan_local),
        preferred_element_type=jnp.float32,
    )
    grad_latlon = summed.astype(jnp.bfloat16).reshape(batch_rows, block_total, seg_len, chan_local)
    kernel_sum = packed[: grad_kernel.size].reshape(grad_kernel.shape)
    mix_sum = packed[grad_kernel.size :].reshape(grad_mix.shape)
    factor = 1.0 / math.sqrt(batch_rows * tile_cells * tile_total)
    return (coupled, grad_latlon, kernel_sum * factor, mix_sum * factor)


def physical_mesh(mesh):
    devices = mesh.devices
    tile_devs = devices[:, 0]
    x_count = len({d.coords[0] for d in tile_devs})
    y_count = len({d.coords[1] for d in tile_devs})
    zl_count = tile_devs.size // (x_count * y_count)
    zh_count = len({d.coords[2] for d in devices[0, :]})
    core_count = devices.shape[1] // zh_count
    shaped = devices.reshape(x_count, zl_count, y_count, zh_count, core_count)
    return Mesh(shaped, TILE + CHAN)


def solution(mesh):
    mesh = physical_mesh(mesh)
    return jax.shard_map(
        body,
        mesh=mesh,
        in_specs=(
            P(None, TILE, None, CHAN),
            P(TILE, None, None),
            P(),
            P(),
            P(),
            P(TILE),
            P(None, None, CHAN),
            P(),
            P(None, TILE, CHAN),
        ),
        out_specs=(
            P(None, TILE, CHAN),
            P(None, TILE, None, CHAN),
            P(None, None, CHAN),
            P(CHAN, None),
        ),
        check_vma=False,
    )
```

```python
import math

import jax
import jax.numpy as jnp
from jax import lax
from jax.sharding import Mesh, PartitionSpec as P

TILE_EDGE = 32
TILE = ("x", "zl", "y")
CHAN = ("zh", "core")


def turn_kernel(kernel, turn, direction):
    turned = jnp.zeros_like(kernel)
    for quarter in range(4):
        turned = turned + jnp.where(
            turn == quarter, jnp.rot90(kernel, direction * quarter, axes=(0, 1)), 0.0
        )
    return turned


def stencil_apply(field, kernel):
    shape_out = (field.shape[0], TILE_EDGE, TILE_EDGE, field.shape[3])
    hidden = jnp.zeros(shape_out, jnp.float32)
    for row_off in range(3):
        for col_off in range(3):
            window = field[
                :, row_off : row_off + TILE_EDGE, col_off : col_off + TILE_EDGE, :
            ].astype(jnp.float32)
            hidden = hidden + kernel[row_off, col_off] * window
    return hidden


def stencil_grads(field, kernel, grad_hidden):
    tap_rows = []
    grad_field = jnp.zeros(field.shape, jnp.float32)
    for row_off in range(3):
        tap_cols = []
        for col_off in range(3):
            window = field[
                :, row_off : row_off + TILE_EDGE, col_off : col_off + TILE_EDGE, :
            ].astype(jnp.float32)
            tap_cols.append(jnp.sum(window * grad_hidden, axis=(0, 1, 2)))
            spread = kernel[row_off, col_off] * grad_hidden
            grad_field = grad_field + jnp.pad(
                spread, ((0, 0), (row_off, 2 - row_off), (col_off, 2 - col_off), (0, 0))
            )
        tap_rows.append(jnp.stack(tap_cols))
    return (jnp.stack(tap_rows), grad_field)


def tile_partial(flat, parts):
    total = flat.shape[0]
    width = -(-total // (parts * 128)) * 128
    rows = jnp.pad(flat, (0, parts * width - total)).reshape(parts, width)
    pieces = lax.all_to_all(rows, TILE, split_axis=0, concat_axis=0, tiled=True)
    return jnp.sum(pieces, axis=0)


def as_word_pair(value):
    high = lax.reduce_precision(value, exponent_bits=8, mantissa_bits=7)
    low = value - high
    return jnp.concatenate([high.astype(jnp.bfloat16), low.astype(jnp.bfloat16)])


def from_word_pair(words):
    width = words.shape[-1] // 2
    return words[..., :width].astype(jnp.float32) + words[..., width:].astype(jnp.float32)


def body(
    latlon,
    remap_weights,
    term_source,
    term_block,
    term_count,
    rotation,
    depthwise,
    pointwise,
    cotangent,
):
    tile_now = lax.axis_index(TILE)
    tile_total = term_source.shape[0]
    chan_now = lax.axis_index(CHAN)
    batch_rows, block_total, seg_len, chan_local = latlon.shape
    terms_max = term_source.shape[1]
    capacity = 3 * terms_max // (2 * tile_total)
    ext_edge = TILE_EDGE + 2
    tile_cells = TILE_EDGE * TILE_EDGE
    flat_rows = batch_rows * tile_cells
    positions = jnp.arange(terms_max, dtype=jnp.int32)
    in_use = positions[None, :] < term_count[:, None]
    mine = in_use & (term_source == tile_now)
    send_rank = jnp.cumsum(mine.astype(jnp.int32), axis=1) - 1
    slot_ids = jnp.arange(capacity, dtype=jnp.int32)
    slot_hits = mine[:, :, None] & (send_rank[:, :, None] == slot_ids[None, None, :])
    slot_filled = jnp.any(slot_hits, axis=1).reshape(-1)
    slot_block = jnp.sum(jnp.where(slot_hits, term_block[:, :, None], 0), axis=1).reshape(-1)
    outgoing = jnp.take(latlon, slot_block, axis=1)
    outgoing = jnp.where(slot_filled[None, :, None, None], outgoing, jnp.zeros((), latlon.dtype))
    own_source = lax.dynamic_index_in_dim(term_source, tile_now, 0, keepdims=False)
    own_count = lax.dynamic_index_in_dim(term_count, tile_now, 0, keepdims=False)
    own_use = positions < own_count
    same_source = (
        (own_source[None, :] == own_source[:, None])
        & own_use[None, :]
        & (positions[None, :] <= positions[:, None])
    )
    own_rank = jnp.sum(same_source.astype(jnp.int32), axis=1) - 1
    recv_slot = jnp.where(own_use, own_source * capacity + own_rank, 0)
    return_slot = jnp.where(own_use, own_source * capacity + own_rank, tile_total * capacity)
    weights = remap_weights[0]
    ext_cells = weights.shape[0]
    term_pts = weights.shape[1]
    arrived = lax.all_to_all(outgoing, TILE, split_axis=1, concat_axis=1, tiled=True)
    picked = jnp.take(arrived, recv_slot, axis=1)
    picked = jnp.where(own_use[None, :, None, None], picked, jnp.zeros((), arrived.dtype))
    picked = picked.reshape(picked.shape[0], term_pts, chan_local)
    mapped = jnp.einsum("pk,bkc->bpc", weights, picked, preferred_element_type=jnp.float32)
    remapped = mapped.astype(jnp.bfloat16)
    field = remapped.reshape(batch_rows, ext_edge, ext_edge, chan_local)
    turn = rotation[0]
    kernel = turn_kernel(depthwise.astype(jnp.float32), turn, 1)
    hidden = stencil_apply(field, kernel)
    active = jax.nn.silu(hidden).astype(jnp.bfloat16).reshape(flat_rows, chan_local)
    own_rows = lax.dynamic_slice_in_dim(pointwise, chan_now * chan_local, chan_local, 0)
    own_cols = lax.dynamic_slice_in_dim(pointwise, chan_now * chan_local, chan_local, 1)
    active_all = lax.all_gather(active, CHAN, axis=1, tiled=True)
    mixed = jnp.dot(active_all, own_cols, preferred_element_type=jnp.float32)
    coupled = mixed.astype(jnp.bfloat16).reshape(batch_rows, tile_cells, chan_local)
    upstream = cotangent.reshape(flat_rows, chan_local)
    piece = lax.all_gather(upstream, CHAN, axis=1, tiled=True)
    grad_active = lax.dot_general(
        piece, own_rows, (((1,), (1,)), ((), ())), preferred_element_type=jnp.float32
    )
    block_grad = lax.dot_general(
        active, piece, (((0,), (0,)), ((), ())), preferred_element_type=jnp.float32
    )
    grad_mix = block_grad
    grad_active, grad_mix = (grad_active, grad_mix)
    sigma = jax.nn.sigmoid(hidden)
    grad_hidden = grad_active.reshape(hidden.shape) * sigma * (1.0 + hidden * (1.0 - sigma))
    grad_turned, grad_field = stencil_grads(field, kernel, grad_hidden)
    grad_field = grad_field.astype(jnp.bfloat16).reshape(batch_rows, ext_cells, chan_local)
    grad_terms = jnp.einsum("pk,bpc->bkc", weights, grad_field, preferred_element_type=jnp.float32)
    grad_terms = grad_terms.reshape(batch_rows, terms_max, seg_len, chan_local)
    grad_terms = jnp.where(own_use[None, :, None, None], grad_terms, 0.0).astype(jnp.bfloat16)
    slot_all = jnp.arange(tile_total * capacity, dtype=jnp.int32)
    place = (slot_all[:, None] == return_slot[None, :]).astype(jnp.bfloat16)
    returning = jnp.einsum(
        "st,btc->bsc", place, grad_terms.reshape(batch_rows, terms_max, seg_len * chan_local),
        preferred_element_type=jnp.float32,
    ).astype(jnp.bfloat16).reshape(batch_rows, tile_total * capacity, seg_len, chan_local)
    landing = jnp.where(slot_filled, slot_block, block_total)
    grad_kernel = turn_kernel(grad_turned, turn, -1)
    packed = jnp.concatenate([grad_kernel.reshape(-1), grad_mix.reshape(-1)])
    my_slot = tile_partial(packed, tile_total)
    slot_words = as_word_pair(my_slot)
    unit = seg_len * chan_local
    word_rows = -(-slot_words.shape[0] // unit)
    slot_words = jnp.pad(slot_words, (0, word_rows * unit - slot_words.shape[0]))
    slot_words = slot_words.reshape(1, word_rows, seg_len, chan_local)
    payload = jnp.concatenate(
        [
            returning.reshape(tile_total, capacity, seg_len, chan_local),
            jnp.broadcast_to(slot_words, (tile_total, word_rows, seg_len, chan_local)),
        ],
        axis=1,
    ).reshape(batch_rows, tile_total * (capacity + word_rows), seg_len, chan_local)
    arrived_all = lax.all_to_all(payload, TILE, split_axis=1, concat_axis=1, tiled=True)
    arrived_all = arrived_all.reshape(tile_total, capacity + word_rows, seg_len, chan_local)
    arrived = arrived_all[:, :capacity].reshape(batch_rows, tile_total * capacity, seg_len, chan_local)
    words = arrived_all[:, capacity:].reshape(tile_total, word_rows * unit)
    packed = from_word_pair(words[:, : 2 * my_slot.shape[0]]).reshape(-1)[: packed.shape[0]]
    block_ids = jnp.arange(block_total, dtype=jnp.int32)
    gather_back = (block_ids[:, None] == landing[None, :]).astype(jnp.bfloat16)
    summed = jnp.einsum(
        "ks,bsc->bkc", gather_back, arrived.reshape(batch_rows, tile_total * capacity, seg_len * chan_local),
        preferred_element_type=jnp.float32,
    )
    grad_latlon = summed.astype(jnp.bfloat16).reshape(batch_rows, block_total, seg_len, chan_local)
    kernel_sum = packed[: grad_kernel.size].reshape(grad_kernel.shape)
    mix_sum = packed[grad_kernel.size :].reshape(grad_mix.shape)
    factor = 1.0 / math.sqrt(batch_rows * tile_cells * tile_total)
    return (coupled, grad_latlon, kernel_sum * factor, mix_sum * factor)


def physical_mesh(mesh):
    devices = mesh.devices
    tile_devs = devices[:, 0]
    x_count = len({d.coords[0] for d in tile_devs})
    y_count = len({d.coords[1] for d in tile_devs})
    zl_count = tile_devs.size // (x_count * y_count)
    zh_count = len({d.coords[2] for d in devices[0, :]})
    core_count = devices.shape[1] // zh_count
    shaped = devices.reshape(x_count, zl_count, y_count, zh_count, core_count)
    return Mesh(shaped, TILE + CHAN)


def solution(mesh):
    mesh = physical_mesh(mesh)
    return jax.shard_map(
        body,
        mesh=mesh,
        in_specs=(
            P(None, TILE, None, CHAN),
            P(TILE, None, None),
            P(),
            P(),
            P(),
            P(TILE),
            P(None, None, CHAN),
            P(),
            P(None, TILE, CHAN),
        ),
        out_specs=(
            P(None, TILE, CHAN),
            P(None, TILE, None, CHAN),
            P(None, None, CHAN),
            P(CHAN, None),
        ),
        check_vma=False,
    )
```

```python
import math

import jax
import jax.numpy as jnp
from jax import lax
from jax.sharding import Mesh, PartitionSpec as P

TILE_EDGE = 32
TILE = ("x", "zl", "y")
CHAN = ("zh", "core")


def turn_kernel(kernel, turn, direction):
    turned = jnp.zeros_like(kernel)
    for quarter in range(4):
        turned = turned + jnp.where(
            turn == quarter, jnp.rot90(kernel, direction * quarter, axes=(0, 1)), 0.0
        )
    return turned


def stencil_apply(field, kernel):
    shape_out = (field.shape[0], TILE_EDGE, TILE_EDGE, field.shape[3])
    hidden = jnp.zeros(shape_out, jnp.float32)
    for row_off in range(3):
        for col_off in range(3):
            window = field[
                :, row_off : row_off + TILE_EDGE, col_off : col_off + TILE_EDGE, :
            ].astype(jnp.float32)
            hidden = hidden + kernel[row_off, col_off] * window
    return hidden


def stencil_grads(field, kernel, grad_hidden):
    tap_rows = []
    grad_field = jnp.zeros(field.shape, jnp.float32)
    for row_off in range(3):
        tap_cols = []
        for col_off in range(3):
            window = field[
                :, row_off : row_off + TILE_EDGE, col_off : col_off + TILE_EDGE, :
            ].astype(jnp.float32)
            tap_cols.append(jnp.sum(window * grad_hidden, axis=(0, 1, 2)))
            spread = kernel[row_off, col_off] * grad_hidden
            grad_field = grad_field + jnp.pad(
                spread, ((0, 0), (row_off, 2 - row_off), (col_off, 2 - col_off), (0, 0))
            )
        tap_rows.append(jnp.stack(tap_cols))
    return (jnp.stack(tap_rows), grad_field)


def tile_partial(flat, parts):
    total = flat.shape[0]
    width = -(-total // (parts * 128)) * 128
    rows = jnp.pad(flat, (0, parts * width - total)).reshape(parts, width)
    pieces = lax.all_to_all(rows, TILE, split_axis=0, concat_axis=0, tiled=True)
    return jnp.sum(pieces, axis=0)


def as_word_pair(value):
    high = lax.reduce_precision(value, exponent_bits=8, mantissa_bits=7)
    low = value - high
    return jnp.concatenate([high.astype(jnp.bfloat16), low.astype(jnp.bfloat16)])


def from_word_pair(words):
    width = words.shape[-1] // 2
    return words[..., :width].astype(jnp.float32) + words[..., width:].astype(jnp.float32)


def body(
    latlon,
    remap_weights,
    term_source,
    term_block,
    term_count,
    rotation,
    depthwise,
    pointwise,
    cotangent,
):
    tile_now = lax.axis_index(TILE)
    tile_total = term_source.shape[0]
    chan_now = lax.axis_index(CHAN)
    batch_rows, block_total, seg_len, chan_local = latlon.shape
    terms_max = term_source.shape[1]
    capacity = 3 * terms_max // (2 * tile_total)
    ext_edge = TILE_EDGE + 2
    tile_cells = TILE_EDGE * TILE_EDGE
    flat_rows = batch_rows * tile_cells
    positions = jnp.arange(terms_max, dtype=jnp.int32)
    in_use = positions[None, :] < term_count[:, None]
    mine = in_use & (term_source == tile_now)
    send_rank = jnp.cumsum(mine.astype(jnp.int32), axis=1) - 1
    slot_ids = jnp.arange(capacity, dtype=jnp.int32)
    slot_hits = mine[:, :, None] & (send_rank[:, :, None] == slot_ids[None, None, :])
    slot_filled = jnp.any(slot_hits, axis=1).reshape(-1)
    slot_block = jnp.sum(jnp.where(slot_hits, term_block[:, :, None], 0), axis=1).reshape(-1)
    outgoing = jnp.take(latlon, slot_block, axis=1)
    own_source = lax.dynamic_index_in_dim(term_source, tile_now, 0, keepdims=False)
    own_count = lax.dynamic_index_in_dim(term_count, tile_now, 0, keepdims=False)
    own_use = positions < own_count
    same_source = (
        (own_source[None, :] == own_source[:, None])
        & own_use[None, :]
        & (positions[None, :] <= positions[:, None])
    )
    own_rank = jnp.sum(same_source.astype(jnp.int32), axis=1) - 1
    recv_slot = jnp.where(own_use, own_source * capacity + own_rank, 0)
    return_slot = jnp.where(own_use, own_source * capacity + own_rank, tile_total * capacity)
    weights = remap_weights[0]
    ext_cells = weights.shape[0]
    term_pts = weights.shape[1]
    arrived = lax.all_to_all(outgoing, TILE, split_axis=1, concat_axis=1, tiled=True)
    picked = jnp.take(arrived, recv_slot, axis=1)
    picked = jnp.where(own_use[None, :, None, None], picked, jnp.zeros((), arrived.dtype))
    picked = picked.reshape(picked.shape[0], term_pts, chan_local)
    mapped = jnp.einsum("pk,bkc->bpc", weights, picked, preferred_element_type=jnp.float32)
    remapped = mapped.astype(jnp.bfloat16)
    field = remapped.reshape(batch_rows, ext_edge, ext_edge, chan_local)
    turn = rotation[0]
    kernel = turn_kernel(depthwise.astype(jnp.float32), turn, 1)
    hidden = stencil_apply(field, kernel)
    active = jax.nn.silu(hidden).astype(jnp.bfloat16).reshape(flat_rows, chan_local)
    own_rows = lax.dynamic_slice_in_dim(pointwise, chan_now * chan_local, chan_local, 0)
    own_cols = lax.dynamic_slice_in_dim(pointwise, chan_now * chan_local, chan_local, 1)
    active_all = lax.all_gather(active, CHAN, axis=1, tiled=True)
    mixed = jnp.dot(active_all, own_cols, preferred_element_type=jnp.float32)
    coupled = mixed.astype(jnp.bfloat16).reshape(batch_rows, tile_cells, chan_local)
    upstream = cotangent.reshape(flat_rows, chan_local)
    piece = lax.all_gather(upstream, CHAN, axis=1, tiled=True)
    grad_active = lax.dot_general(
        piece, own_rows, (((1,), (1,)), ((), ())), preferred_element_type=jnp.float32
    )
    block_grad = lax.dot_general(
        active, piece, (((0,), (0,)), ((), ())), preferred_element_type=jnp.float32
    )
    grad_mix = block_grad
    grad_active, grad_mix = (grad_active, grad_mix)
    sigma = jax.nn.sigmoid(hidden)
    grad_hidden = grad_active.reshape(hidden.shape) * sigma * (1.0 + hidden * (1.0 - sigma))
    grad_turned, grad_field = stencil_grads(field, kernel, grad_hidden)
    grad_field = grad_field.astype(jnp.bfloat16).reshape(batch_rows, ext_cells, chan_local)
    grad_terms = jnp.einsum("pk,bpc->bkc", weights, grad_field, preferred_element_type=jnp.float32)
    grad_terms = grad_terms.reshape(batch_rows, terms_max, seg_len, chan_local)
    grad_terms = jnp.where(own_use[None, :, None, None], grad_terms, 0.0).astype(jnp.bfloat16)
    slot_all = jnp.arange(tile_total * capacity, dtype=jnp.int32)
    place = (slot_all[:, None] == return_slot[None, :]).astype(jnp.bfloat16)
    returning = jnp.einsum(
        "st,btc->bsc", place, grad_terms.reshape(batch_rows, terms_max, seg_len * chan_local),
        preferred_element_type=jnp.float32,
    ).astype(jnp.bfloat16).reshape(batch_rows, tile_total * capacity, seg_len, chan_local)
    landing = jnp.where(slot_filled, slot_block, block_total)
    grad_kernel = turn_kernel(grad_turned, turn, -1)
    packed = jnp.concatenate([grad_kernel.reshape(-1), grad_mix.reshape(-1)])
    factor = 1.0 / math.sqrt(batch_rows * tile_cells * tile_total)
    exact_scale = float(math.log2(factor)).is_integer()
    if exact_scale:
        packed = packed * factor
    my_slot = tile_partial(packed, tile_total)
    slot_words = as_word_pair(my_slot)
    unit = seg_len * chan_local
    word_rows = -(-slot_words.shape[0] // unit)
    slot_words = jnp.pad(slot_words, (0, word_rows * unit - slot_words.shape[0]))
    slot_words = slot_words.reshape(1, word_rows, seg_len, chan_local)
    payload = jnp.concatenate(
        [
            returning.reshape(tile_total, capacity, seg_len, chan_local),
            jnp.broadcast_to(slot_words, (tile_total, word_rows, seg_len, chan_local)),
        ],
        axis=1,
    ).reshape(batch_rows, tile_total * (capacity + word_rows), seg_len, chan_local)
    arrived_all = lax.all_to_all(payload, TILE, split_axis=1, concat_axis=1, tiled=True)
    arrived_all = arrived_all.reshape(tile_total, capacity + word_rows, seg_len, chan_local)
    arrived = arrived_all[:, :capacity].reshape(batch_rows, tile_total * capacity, seg_len, chan_local)
    words = arrived_all[:, capacity:].reshape(tile_total, word_rows * unit)
    packed = from_word_pair(words[:, : 2 * my_slot.shape[0]]).reshape(-1)[: packed.shape[0]]
    block_ids = jnp.arange(block_total, dtype=jnp.int32)
    gather_back = (block_ids[:, None] == landing[None, :]).astype(jnp.bfloat16)
    summed = lax.dot_general(
        gather_back, arrived.reshape(tile_total * capacity, seg_len * chan_local),
        (((1,), (0,)), ((), ())), preferred_element_type=jnp.float32,
    )
    grad_latlon = summed.astype(jnp.bfloat16).reshape(batch_rows, block_total, seg_len, chan_local)
    kernel_sum = packed[: grad_kernel.size].reshape(grad_kernel.shape)
    mix_sum = packed[grad_kernel.size :].reshape(grad_mix.shape)
    if not exact_scale:
        kernel_sum = kernel_sum * factor
        mix_sum = mix_sum * factor
    return (coupled, grad_latlon, kernel_sum, mix_sum)


def physical_mesh(mesh):
    devices = mesh.devices
    tile_devs = devices[:, 0]
    x_count = len({d.coords[0] for d in tile_devs})
    y_count = len({d.coords[1] for d in tile_devs})
    zl_count = tile_devs.size // (x_count * y_count)
    zh_count = len({d.coords[2] for d in devices[0, :]})
    core_count = devices.shape[1] // zh_count
    shaped = devices.reshape(x_count, zl_count, y_count, zh_count, core_count)
    return Mesh(shaped, TILE + CHAN)


def solution(mesh):
    mesh = physical_mesh(mesh)
    return jax.shard_map(
        body,
        mesh=mesh,
        in_specs=(
            P(None, TILE, None, CHAN),
            P(TILE, None, None),
            P(),
            P(),
            P(),
            P(TILE),
            P(None, None, CHAN),
            P(),
            P(None, TILE, CHAN),
        ),
        out_specs=(
            P(None, TILE, CHAN),
            P(None, TILE, None, CHAN),
            P(None, None, CHAN),
            P(CHAN, None),
        ),
        check_vma=False,
    )
```

```python
import math

import jax
import jax.numpy as jnp
from jax import lax
from jax.sharding import Mesh, PartitionSpec as P

TILE_EDGE = 32
TILE = ("x", "zl", "y")
CHAN = ("zh", "core")


def turn_kernel(kernel, turn, direction):
    turned = jnp.zeros_like(kernel)
    for quarter in range(4):
        turned = turned + jnp.where(
            turn == quarter, jnp.rot90(kernel, direction * quarter, axes=(0, 1)), 0.0
        )
    return turned


def stencil_apply(field, kernel):
    shape_out = (field.shape[0], TILE_EDGE, TILE_EDGE, field.shape[3])
    hidden = jnp.zeros(shape_out, jnp.float32)
    for row_off in range(3):
        for col_off in range(3):
            window = field[
                :, row_off : row_off + TILE_EDGE, col_off : col_off + TILE_EDGE, :
            ].astype(jnp.float32)
            hidden = hidden + kernel[row_off, col_off] * window
    return hidden


def stencil_grads(field, kernel, grad_hidden):
    tap_rows = []
    grad_field = jnp.zeros(field.shape, jnp.float32)
    for row_off in range(3):
        tap_cols = []
        for col_off in range(3):
            window = field[
                :, row_off : row_off + TILE_EDGE, col_off : col_off + TILE_EDGE, :
            ].astype(jnp.float32)
            tap_cols.append(jnp.sum(window * grad_hidden, axis=(0, 1, 2)))
            spread = kernel[row_off, col_off] * grad_hidden
            grad_field = grad_field + jnp.pad(
                spread, ((0, 0), (row_off, 2 - row_off), (col_off, 2 - col_off), (0, 0))
            )
        tap_rows.append(jnp.stack(tap_cols))
    return (jnp.stack(tap_rows), grad_field)


def tile_partial(flat, parts):
    total = flat.shape[0]
    width = -(-total // (parts * 128)) * 128
    rows = jnp.pad(flat, (0, parts * width - total)).reshape(parts, width)
    pieces = lax.all_to_all(rows, TILE, split_axis=0, concat_axis=0, tiled=True)
    return jnp.sum(pieces, axis=0)


def as_word_pair(value):
    high = lax.reduce_precision(value, exponent_bits=8, mantissa_bits=7)
    low = value - high
    return jnp.concatenate([high.astype(jnp.bfloat16), low.astype(jnp.bfloat16)])


def from_word_pair(words):
    width = words.shape[-1] // 2
    return words[..., :width].astype(jnp.float32) + words[..., width:].astype(jnp.float32)


def body(
    latlon,
    remap_weights,
    term_source,
    term_block,
    term_count,
    rotation,
    depthwise,
    pointwise,
    cotangent,
):
    tile_now = lax.axis_index(TILE)
    tile_total = term_source.shape[0]
    chan_now = lax.axis_index(CHAN)
    batch_rows, block_total, seg_len, chan_local = latlon.shape
    terms_max = term_source.shape[1]
    capacity = 3 * terms_max // (2 * tile_total)
    ext_edge = TILE_EDGE + 2
    tile_cells = TILE_EDGE * TILE_EDGE
    flat_rows = batch_rows * tile_cells
    positions = jnp.arange(terms_max, dtype=jnp.int32)
    in_use = positions[None, :] < term_count[:, None]
    mine = in_use & (term_source == tile_now)
    send_rank = jnp.cumsum(mine.astype(jnp.int32), axis=1) - 1
    slot_ids = jnp.arange(capacity, dtype=jnp.int32)
    slot_hits = mine[:, :, None] & (send_rank[:, :, None] == slot_ids[None, None, :])
    slot_filled = jnp.any(slot_hits, axis=1).reshape(-1)
    slot_block = jnp.sum(jnp.where(slot_hits, term_block[:, :, None], 0), axis=1).reshape(-1)
    outgoing = jnp.take(latlon, slot_block, axis=1)
    own_source = lax.dynamic_index_in_dim(term_source, tile_now, 0, keepdims=False)
    own_count = lax.dynamic_index_in_dim(term_count, tile_now, 0, keepdims=False)
    own_use = positions < own_count
    same_source = (
        (own_source[None, :] == own_source[:, None])
        & own_use[None, :]
        & (positions[None, :] <= positions[:, None])
    )
    own_rank = jnp.sum(same_source.astype(jnp.int32), axis=1) - 1
    recv_slot = jnp.where(own_use, own_source * capacity + own_rank, 0)
    return_slot = jnp.where(own_use, own_source * capacity + own_rank, tile_total * capacity)
    weights = remap_weights[0]
    ext_cells = weights.shape[0]
    term_pts = weights.shape[1]
    arrived = lax.all_to_all(outgoing, TILE, split_axis=1, concat_axis=1, tiled=True)
    picked = jnp.take(arrived, recv_slot, axis=1)
    picked = jnp.where(own_use[None, :, None, None], picked, jnp.zeros((), arrived.dtype))
    picked = picked.reshape(picked.shape[0], term_pts, chan_local)
    mapped = jnp.einsum("pk,bkc->bpc", weights, picked, preferred_element_type=jnp.float32)
    remapped = mapped.astype(jnp.bfloat16)
    field = remapped.reshape(batch_rows, ext_edge, ext_edge, chan_local)
    turn = rotation[0]
    kernel = turn_kernel(depthwise.astype(jnp.float32), turn, 1)
    hidden = stencil_apply(field, kernel)
    active = jax.nn.silu(hidden).astype(jnp.bfloat16).reshape(flat_rows, chan_local)
    own_rows = lax.dynamic_slice_in_dim(pointwise, chan_now * chan_local, chan_local, 0)
    own_cols = lax.dynamic_slice_in_dim(pointwise, chan_now * chan_local, chan_local, 1)
    chan_total = pointwise.shape[0] // chan_local
    blocks = [active]
    for shift in range(1, chan_total):
        pairs = [(src, (src + shift) % chan_total) for src in range(chan_total)]
        blocks.append(lax.ppermute(active, CHAN, pairs))
    active_all = jnp.concatenate(blocks, axis=1)
    chan_order = (chan_now - jnp.arange(chan_total, dtype=jnp.int32)) % chan_total
    col_block = lax.dynamic_slice_in_dim(pointwise, chan_now * chan_local, chan_local, 1)
    mixing_rows = jnp.take(col_block.reshape(chan_total, chan_local, chan_local), chan_order, axis=0)
    mixing_rows = mixing_rows.reshape(chan_total * chan_local, chan_local)
    mixed = jnp.dot(active_all, mixing_rows, preferred_element_type=jnp.float32)
    coupled = mixed.astype(jnp.bfloat16).reshape(batch_rows, tile_cells, chan_local)
    upstream = cotangent.reshape(flat_rows, chan_local)
    piece = lax.all_gather(upstream, CHAN, axis=1, tiled=True)
    grad_active = lax.dot_general(
        piece, own_rows, (((1,), (1,)), ((), ())), preferred_element_type=jnp.float32
    )
    block_grad = lax.dot_general(
        active, piece, (((0,), (0,)), ((), ())), preferred_element_type=jnp.float32
    )
    grad_mix = block_grad
    grad_active, grad_mix = (grad_active, grad_mix)
    sigma = jax.nn.sigmoid(hidden)
    grad_hidden = grad_active.reshape(hidden.shape) * sigma * (1.0 + hidden * (1.0 - sigma))
    grad_turned, grad_field = stencil_grads(field, kernel, grad_hidden)
    grad_field = grad_field.astype(jnp.bfloat16).reshape(batch_rows, ext_cells, chan_local)
    grad_terms = jnp.einsum("pk,bpc->bkc", weights, grad_field, preferred_element_type=jnp.float32)
    grad_terms = grad_terms.reshape(batch_rows, terms_max, seg_len, chan_local)
    grad_terms = jnp.where(own_use[None, :, None, None], grad_terms, 0.0).astype(jnp.bfloat16)
    slot_all = jnp.arange(tile_total * capacity, dtype=jnp.int32)
    place = (slot_all[:, None] == return_slot[None, :]).astype(jnp.bfloat16)
    returning = jnp.einsum(
        "st,btc->bsc", place, grad_terms.reshape(batch_rows, terms_max, seg_len * chan_local),
        preferred_element_type=jnp.float32,
    ).astype(jnp.bfloat16).reshape(batch_rows, tile_total * capacity, seg_len, chan_local)
    landing = jnp.where(slot_filled, slot_block, block_total)
    grad_kernel = turn_kernel(grad_turned, turn, -1)
    packed = jnp.concatenate([grad_kernel.reshape(-1), grad_mix.reshape(-1)])
    factor = 1.0 / math.sqrt(batch_rows * tile_cells * tile_total)
    exact_scale = float(math.log2(factor)).is_integer()
    if exact_scale:
        packed = packed * factor
    my_slot = tile_partial(packed, tile_total)
    slot_words = as_word_pair(my_slot)
    unit = seg_len * chan_local
    word_rows = -(-slot_words.shape[0] // unit)
    slot_words = jnp.pad(slot_words, (0, word_rows * unit - slot_words.shape[0]))
    slot_words = slot_words.reshape(1, word_rows, seg_len, chan_local)
    payload = jnp.concatenate(
        [
            returning.reshape(tile_total, capacity, seg_len, chan_local),
            jnp.broadcast_to(slot_words, (tile_total, word_rows, seg_len, chan_local)),
        ],
        axis=1,
    ).reshape(batch_rows, tile_total * (capacity + word_rows), seg_len, chan_local)
    arrived_all = lax.all_to_all(payload, TILE, split_axis=1, concat_axis=1, tiled=True)
    arrived_all = arrived_all.reshape(tile_total, capacity + word_rows, seg_len, chan_local)
    arrived = arrived_all[:, :capacity].reshape(batch_rows, tile_total * capacity, seg_len, chan_local)
    words = arrived_all[:, capacity:].reshape(tile_total, word_rows * unit)
    packed = from_word_pair(words[:, : 2 * my_slot.shape[0]]).reshape(-1)[: packed.shape[0]]
    block_ids = jnp.arange(block_total, dtype=jnp.int32)
    gather_back = (block_ids[:, None] == landing[None, :]).astype(jnp.bfloat16)
    summed = lax.dot_general(
        gather_back, arrived.reshape(tile_total * capacity, seg_len * chan_local),
        (((1,), (0,)), ((), ())), preferred_element_type=jnp.float32,
    )
    grad_latlon = summed.astype(jnp.bfloat16).reshape(batch_rows, block_total, seg_len, chan_local)
    kernel_sum = packed[: grad_kernel.size].reshape(grad_kernel.shape)
    mix_sum = packed[grad_kernel.size :].reshape(grad_mix.shape)
    if not exact_scale:
        kernel_sum = kernel_sum * factor
        mix_sum = mix_sum * factor
    return (coupled, grad_latlon, kernel_sum, mix_sum)


def physical_mesh(mesh):
    devices = mesh.devices
    tile_devs = devices[:, 0]
    x_count = len({d.coords[0] for d in tile_devs})
    y_count = len({d.coords[1] for d in tile_devs})
    zl_count = tile_devs.size // (x_count * y_count)
    zh_count = len({d.coords[2] for d in devices[0, :]})
    core_count = devices.shape[1] // zh_count
    shaped = devices.reshape(x_count, zl_count, y_count, zh_count, core_count)
    return Mesh(shaped, TILE + CHAN)


def solution(mesh):
    mesh = physical_mesh(mesh)
    return jax.shard_map(
        body,
        mesh=mesh,
        in_specs=(
            P(None, TILE, None, CHAN),
            P(TILE, None, None),
            P(),
            P(),
            P(),
            P(TILE),
            P(None, None, CHAN),
            P(),
            P(None, TILE, CHAN),
        ),
        out_specs=(
            P(None, TILE, CHAN),
            P(None, TILE, None, CHAN),
            P(None, None, CHAN),
            P(CHAN, None),
        ),
        check_vma=False,
    )
```

```python
import math

import jax
import jax.numpy as jnp
from jax import lax
from jax.sharding import Mesh, PartitionSpec as P

TILE_EDGE = 32
TILE = ("x", "zl", "y")
CHAN = ("zh", "core")


def turn_kernel(kernel, turn, direction):
    turned = jnp.zeros_like(kernel)
    for quarter in range(4):
        turned = turned + jnp.where(
            turn == quarter, jnp.rot90(kernel, direction * quarter, axes=(0, 1)), 0.0
        )
    return turned


def stencil_apply(field, kernel):
    shape_out = (field.shape[0], TILE_EDGE, TILE_EDGE, field.shape[3])
    hidden = jnp.zeros(shape_out, jnp.float32)
    for row_off in range(3):
        for col_off in range(3):
            window = field[
                :, row_off : row_off + TILE_EDGE, col_off : col_off + TILE_EDGE, :
            ].astype(jnp.float32)
            hidden = hidden + kernel[row_off, col_off] * window
    return hidden


def stencil_grads(field, kernel, grad_hidden):
    tap_rows = []
    grad_field = jnp.zeros(field.shape, jnp.float32)
    for row_off in range(3):
        tap_cols = []
        for col_off in range(3):
            window = field[
                :, row_off : row_off + TILE_EDGE, col_off : col_off + TILE_EDGE, :
            ].astype(jnp.float32)
            tap_cols.append(jnp.sum(window * grad_hidden, axis=(0, 1, 2)))
            spread = kernel[row_off, col_off] * grad_hidden
            grad_field = grad_field + jnp.pad(
                spread, ((0, 0), (row_off, 2 - row_off), (col_off, 2 - col_off), (0, 0))
            )
        tap_rows.append(jnp.stack(tap_cols))
    return (jnp.stack(tap_rows), grad_field)


def tile_partial(flat, parts):
    total = flat.shape[0]
    width = -(-total // (parts * 128)) * 128
    rows = jnp.pad(flat, (0, parts * width - total)).reshape(parts, width)
    pieces = lax.all_to_all(rows, TILE, split_axis=0, concat_axis=0, tiled=True)
    return jnp.sum(pieces, axis=0)


def as_word_pair(value):
    high = lax.reduce_precision(value, exponent_bits=8, mantissa_bits=7)
    low = value - high
    return jnp.concatenate([high.astype(jnp.bfloat16), low.astype(jnp.bfloat16)])


def from_word_pair(words):
    width = words.shape[-1] // 2
    return words[..., :width].astype(jnp.float32) + words[..., width:].astype(jnp.float32)


def body(
    latlon,
    remap_weights,
    term_source,
    term_block,
    term_count,
    rotation,
    depthwise,
    pointwise,
    cotangent,
):
    tile_now = lax.axis_index(TILE)
    tile_total = term_source.shape[0]
    chan_now = lax.axis_index(CHAN)
    batch_rows, block_total, seg_len, chan_local = latlon.shape
    terms_max = term_source.shape[1]
    capacity = 3 * terms_max // (2 * tile_total)
    ext_edge = TILE_EDGE + 2
    tile_cells = TILE_EDGE * TILE_EDGE
    flat_rows = batch_rows * tile_cells
    positions = jnp.arange(terms_max, dtype=jnp.int32)
    in_use = positions[None, :] < term_count[:, None]
    mine = in_use & (term_source == tile_now)
    send_rank = jnp.cumsum(mine.astype(jnp.int32), axis=1) - 1
    slot_ids = jnp.arange(capacity, dtype=jnp.int32)
    slot_hits = mine[:, :, None] & (send_rank[:, :, None] == slot_ids[None, None, :])
    slot_filled = jnp.any(slot_hits, axis=1).reshape(-1)
    slot_block = jnp.sum(jnp.where(slot_hits, term_block[:, :, None], 0), axis=1).reshape(-1)
    row_width = batch_rows * seg_len
    latlon_rows = jnp.moveaxis(latlon, 0, 1).reshape(block_total, row_width, chan_local)
    outgoing = jnp.take(latlon_rows, slot_block, axis=0, mode="clip")
    own_source = lax.dynamic_index_in_dim(term_source, tile_now, 0, keepdims=False)
    own_count = lax.dynamic_index_in_dim(term_count, tile_now, 0, keepdims=False)
    own_use = positions < own_count
    same_source = (
        (own_source[None, :] == own_source[:, None])
        & own_use[None, :]
        & (positions[None, :] <= positions[:, None])
    )
    own_rank = jnp.sum(same_source.astype(jnp.int32), axis=1) - 1
    recv_slot = jnp.where(own_use, own_source * capacity + own_rank, 0)
    return_slot = jnp.where(own_use, own_source * capacity + own_rank, tile_total * capacity)
    weights = remap_weights[0]
    ext_cells = weights.shape[0]
    term_pts = weights.shape[1]
    arrived = lax.all_to_all(outgoing, TILE, split_axis=0, concat_axis=0, tiled=True)
    picked = jnp.take(arrived, recv_slot, axis=0, mode="clip")
    picked = jnp.where(own_use[:, None, None], picked, jnp.zeros((), arrived.dtype))
    picked = picked.reshape(terms_max, batch_rows, seg_len, chan_local)
    picked = jnp.moveaxis(picked, 1, 0).reshape(batch_rows, term_pts, chan_local)
    mapped = jnp.einsum("pk,bkc->bpc", weights, picked, preferred_element_type=jnp.float32)
    remapped = mapped.astype(jnp.bfloat16)
    field = remapped.reshape(batch_rows, ext_edge, ext_edge, chan_local)
    turn = rotation[0]
    kernel = turn_kernel(depthwise.astype(jnp.float32), turn, 1)
    hidden = stencil_apply(field, kernel)
    active = jax.nn.silu(hidden).astype(jnp.bfloat16).reshape(flat_rows, chan_local)
    own_rows = lax.dynamic_slice_in_dim(pointwise, chan_now * chan_local, chan_local, 0)
    own_cols = lax.dynamic_slice_in_dim(pointwise, chan_now * chan_local, chan_local, 1)
    active_all = lax.all_gather(active, CHAN, axis=1, tiled=True)
    mixed = jnp.dot(active_all, own_cols, preferred_element_type=jnp.float32)
    coupled = mixed.astype(jnp.bfloat16).reshape(batch_rows, tile_cells, chan_local)
    upstream = cotangent.reshape(flat_rows, chan_local)
    piece = lax.all_gather(upstream, CHAN, axis=1, tiled=True)
    grad_active = lax.dot_general(
        piece, own_rows, (((1,), (1,)), ((), ())), preferred_element_type=jnp.float32
    )
    block_grad = lax.dot_general(
        active, piece, (((0,), (0,)), ((), ())), preferred_element_type=jnp.float32
    )
    grad_mix = block_grad
    grad_active, grad_mix = (grad_active, grad_mix)
    sigma = jax.nn.sigmoid(hidden)
    grad_hidden = grad_active.reshape(hidden.shape) * sigma * (1.0 + hidden * (1.0 - sigma))
    grad_turned, grad_field = stencil_grads(field, kernel, grad_hidden)
    grad_field = grad_field.astype(jnp.bfloat16).reshape(batch_rows, ext_cells, chan_local)
    grad_terms = jnp.einsum("pk,bpc->bkc", weights, grad_field, preferred_element_type=jnp.float32)
    grad_terms = grad_terms.reshape(batch_rows, terms_max, seg_len, chan_local)
    grad_terms = jnp.where(own_use[None, :, None, None], grad_terms, 0.0).astype(jnp.bfloat16)
    slot_all = jnp.arange(tile_total * capacity, dtype=jnp.int32)
    place = (slot_all[:, None] == return_slot[None, :]).astype(jnp.bfloat16)
    returning = jnp.einsum(
        "st,btc->bsc", place, grad_terms.reshape(batch_rows, terms_max, seg_len * chan_local),
        preferred_element_type=jnp.float32,
    ).astype(jnp.bfloat16).reshape(batch_rows, tile_total * capacity, seg_len, chan_local)
    landing = jnp.where(slot_filled, slot_block, block_total)
    grad_kernel = turn_kernel(grad_turned, turn, -1)
    packed = jnp.concatenate([grad_kernel.reshape(-1), grad_mix.reshape(-1)])
    factor = 1.0 / math.sqrt(batch_rows * tile_cells * tile_total)
    exact_scale = float(math.log2(factor)).is_integer()
    if exact_scale:
        packed = packed * factor
    my_slot = tile_partial(packed, tile_total)
    slot_words = as_word_pair(my_slot)
    unit = seg_len * chan_local
    word_rows = -(-slot_words.shape[0] // unit)
    slot_words = jnp.pad(slot_words, (0, word_rows * unit - slot_words.shape[0]))
    slot_words = slot_words.reshape(1, word_rows, seg_len, chan_local)
    payload = jnp.concatenate(
        [
            returning.reshape(tile_total, capacity, seg_len, chan_local),
            jnp.broadcast_to(slot_words, (tile_total, word_rows, seg_len, chan_local)),
        ],
        axis=1,
    ).reshape(batch_rows, tile_total * (capacity + word_rows), seg_len, chan_local)
    arrived_all = lax.all_to_all(payload, TILE, split_axis=1, concat_axis=1, tiled=True)
    arrived_all = arrived_all.reshape(tile_total, capacity + word_rows, seg_len, chan_local)
    arrived = arrived_all[:, :capacity].reshape(batch_rows, tile_total * capacity, seg_len, chan_local)
    words = arrived_all[:, capacity:].reshape(tile_total, word_rows * unit)
    packed = from_word_pair(words[:, : 2 * my_slot.shape[0]]).reshape(-1)[: packed.shape[0]]
    block_ids = jnp.arange(block_total, dtype=jnp.int32)
    gather_back = (block_ids[:, None] == landing[None, :]).astype(jnp.bfloat16)
    summed = lax.dot_general(
        gather_back, arrived.reshape(tile_total * capacity, seg_len * chan_local),
        (((1,), (0,)), ((), ())), preferred_element_type=jnp.float32,
    )
    grad_latlon = summed.astype(jnp.bfloat16).reshape(batch_rows, block_total, seg_len, chan_local)
    kernel_sum = packed[: grad_kernel.size].reshape(grad_kernel.shape)
    mix_sum = packed[grad_kernel.size :].reshape(grad_mix.shape)
    if not exact_scale:
        kernel_sum = kernel_sum * factor
        mix_sum = mix_sum * factor
    return (coupled, grad_latlon, kernel_sum, mix_sum)


def physical_mesh(mesh):
    devices = mesh.devices
    tile_devs = devices[:, 0]
    x_count = len({d.coords[0] for d in tile_devs})
    y_count = len({d.coords[1] for d in tile_devs})
    zl_count = tile_devs.size // (x_count * y_count)
    zh_count = len({d.coords[2] for d in devices[0, :]})
    core_count = devices.shape[1] // zh_count
    shaped = devices.reshape(x_count, zl_count, y_count, zh_count, core_count)
    return Mesh(shaped, TILE + CHAN)


def solution(mesh):
    mesh = physical_mesh(mesh)
    return jax.shard_map(
        body,
        mesh=mesh,
        in_specs=(
            P(None, TILE, None, CHAN),
            P(TILE, None, None),
            P(),
            P(),
            P(),
            P(TILE),
            P(None, None, CHAN),
            P(),
            P(None, TILE, CHAN),
        ),
        out_specs=(
            P(None, TILE, CHAN),
            P(None, TILE, None, CHAN),
            P(None, None, CHAN),
            P(CHAN, None),
        ),
        check_vma=False,
    )
```

```python
import math

import jax
import jax.numpy as jnp
from jax import lax
from jax.sharding import Mesh, PartitionSpec as P

TILE_EDGE = 32
TILE = ("x", "zl", "y")
CHAN = ("zh", "core")


def turn_kernel(kernel, turn, direction):
    turned = jnp.zeros_like(kernel)
    for quarter in range(4):
        turned = turned + jnp.where(
            turn == quarter, jnp.rot90(kernel, direction * quarter, axes=(0, 1)), 0.0
        )
    return turned


def stencil_apply(field, kernel):
    shape_out = (field.shape[0], TILE_EDGE, TILE_EDGE, field.shape[3])
    hidden = jnp.zeros(shape_out, jnp.float32)
    for row_off in range(3):
        for col_off in range(3):
            window = field[
                :, row_off : row_off + TILE_EDGE, col_off : col_off + TILE_EDGE, :
            ].astype(jnp.float32)
            hidden = hidden + kernel[row_off, col_off] * window
    return hidden


def stencil_grads(field, kernel, grad_hidden):
    tap_rows = []
    grad_field = jnp.zeros(field.shape, jnp.float32)
    for row_off in range(3):
        tap_cols = []
        for col_off in range(3):
            window = field[
                :, row_off : row_off + TILE_EDGE, col_off : col_off + TILE_EDGE, :
            ].astype(jnp.float32)
            tap_cols.append(jnp.sum(window * grad_hidden, axis=(0, 1, 2)))
            spread = kernel[row_off, col_off] * grad_hidden
            grad_field = grad_field + jnp.pad(
                spread, ((0, 0), (row_off, 2 - row_off), (col_off, 2 - col_off), (0, 0))
            )
        tap_rows.append(jnp.stack(tap_cols))
    return (jnp.stack(tap_rows), grad_field)


def tile_partial(flat, parts):
    total = flat.shape[0]
    width = -(-total // (parts * 128)) * 128
    rows = jnp.pad(flat, (0, parts * width - total)).reshape(parts, width)
    pieces = lax.all_to_all(rows, TILE, split_axis=0, concat_axis=0, tiled=True)
    return jnp.sum(pieces, axis=0)


def as_word_pair(value):
    high = lax.reduce_precision(value, exponent_bits=8, mantissa_bits=7)
    low = value - high
    return jnp.concatenate([high.astype(jnp.bfloat16), low.astype(jnp.bfloat16)])


def from_word_pair(words):
    width = words.shape[-1] // 2
    return words[..., :width].astype(jnp.float32) + words[..., width:].astype(jnp.float32)


def body(
    latlon,
    remap_weights,
    term_source,
    term_block,
    term_count,
    rotation,
    depthwise,
    pointwise,
    cotangent,
):
    tile_now = lax.axis_index(TILE)
    tile_total = term_source.shape[0]
    chan_now = lax.axis_index(CHAN)
    batch_rows, block_total, seg_len, chan_local = latlon.shape
    terms_max = term_source.shape[1]
    capacity = 3 * terms_max // (2 * tile_total)
    ext_edge = TILE_EDGE + 2
    tile_cells = TILE_EDGE * TILE_EDGE
    flat_rows = batch_rows * tile_cells
    positions = jnp.arange(terms_max, dtype=jnp.int32)
    in_use = positions[None, :] < term_count[:, None]
    mine = in_use & (term_source == tile_now)
    send_rank = jnp.cumsum(mine.astype(jnp.int32), axis=1) - 1
    slot_ids = jnp.arange(capacity, dtype=jnp.int32)
    slot_hits = mine[:, :, None] & (send_rank[:, :, None] == slot_ids[None, None, :])
    slot_filled = jnp.any(slot_hits, axis=1).reshape(-1)
    slot_block = jnp.sum(jnp.where(slot_hits, term_block[:, :, None], 0), axis=1).reshape(-1)
    row_width = batch_rows * seg_len
    latlon_rows = jnp.moveaxis(latlon, 0, 1).reshape(block_total, row_width, chan_local)
    outgoing = jnp.take(latlon_rows, slot_block, axis=0, mode="clip")
    own_source = lax.dynamic_index_in_dim(term_source, tile_now, 0, keepdims=False)
    own_count = lax.dynamic_index_in_dim(term_count, tile_now, 0, keepdims=False)
    own_use = positions < own_count
    same_source = (
        (own_source[None, :] == own_source[:, None])
        & own_use[None, :]
        & (positions[None, :] <= positions[:, None])
    )
    own_rank = jnp.sum(same_source.astype(jnp.int32), axis=1) - 1
    recv_slot = jnp.where(own_use, own_source * capacity + own_rank, 0)
    return_slot = jnp.where(own_use, own_source * capacity + own_rank, tile_total * capacity)
    weights = remap_weights[0]
    ext_cells = weights.shape[0]
    term_pts = weights.shape[1]
    arrived = lax.all_to_all(outgoing, TILE, split_axis=0, concat_axis=0, tiled=True)
    picked = jnp.take(arrived, recv_slot, axis=0, mode="clip")
    picked = jnp.where(own_use[:, None, None], picked, jnp.zeros((), arrived.dtype))
    picked = picked.reshape(terms_max, batch_rows, seg_len, chan_local)
    picked = jnp.moveaxis(picked, 1, 0).reshape(batch_rows, term_pts, chan_local)
    mapped = jnp.einsum("pk,bkc->bpc", weights, picked, preferred_element_type=jnp.float32)
    remapped = mapped.astype(jnp.bfloat16)
    field = remapped.reshape(batch_rows, ext_edge, ext_edge, chan_local)
    turn = rotation[0]
    kernel = turn_kernel(depthwise.astype(jnp.float32), turn, 1)
    hidden = stencil_apply(field, kernel)
    active = jax.nn.silu(hidden).astype(jnp.bfloat16).reshape(flat_rows, chan_local)
    own_rows = lax.dynamic_slice_in_dim(pointwise, chan_now * chan_local, chan_local, 0)
    own_cols = lax.dynamic_slice_in_dim(pointwise, chan_now * chan_local, chan_local, 1)
    active_all = lax.all_gather(active, CHAN, axis=1, tiled=True)
    mixed = jnp.dot(active_all, own_cols, preferred_element_type=jnp.float32)
    coupled = mixed.astype(jnp.bfloat16).reshape(batch_rows, tile_cells, chan_local)
    upstream = cotangent.reshape(flat_rows, chan_local)
    piece = lax.all_gather(upstream, CHAN, axis=1, tiled=True)
    grad_active = lax.dot_general(
        piece, own_rows, (((1,), (1,)), ((), ())), preferred_element_type=jnp.float32
    )
    block_grad = lax.dot_general(
        active, piece, (((0,), (0,)), ((), ())), preferred_element_type=jnp.float32
    )
    grad_mix = block_grad
    grad_active, grad_mix = (grad_active, grad_mix)
    sigma = jax.nn.sigmoid(hidden)
    grad_hidden = grad_active.reshape(hidden.shape) * sigma * (1.0 + hidden * (1.0 - sigma))
    grad_turned, grad_field = stencil_grads(field, kernel, grad_hidden)
    grad_field = grad_field.astype(jnp.bfloat16).reshape(batch_rows, ext_cells, chan_local)
    grad_terms = jnp.einsum("pk,bpc->bkc", weights, grad_field, preferred_element_type=jnp.float32)
    grad_terms = grad_terms.reshape(batch_rows, terms_max, seg_len, chan_local)
    grad_terms = jnp.where(own_use[None, :, None, None], grad_terms, 0.0).astype(jnp.bfloat16)
    slot_all = jnp.arange(tile_total * capacity, dtype=jnp.int32)
    place = (slot_all[:, None] == return_slot[None, :]).astype(jnp.bfloat16)
    returning = jnp.einsum(
        "st,btc->bsc", place, grad_terms.reshape(batch_rows, terms_max, seg_len * chan_local),
        preferred_element_type=jnp.float32,
    ).astype(jnp.bfloat16).reshape(batch_rows, tile_total * capacity, seg_len, chan_local)
    landing = jnp.where(slot_filled, slot_block, block_total)
    grad_kernel = turn_kernel(grad_turned, turn, -1)
    packed = jnp.concatenate([grad_kernel.reshape(-1), grad_mix.reshape(-1)])
    factor = 1.0 / math.sqrt(batch_rows * tile_cells * tile_total)
    exact_scale = float(math.log2(factor)).is_integer()
    if exact_scale:
        packed = packed * factor
    my_slot = tile_partial(packed, tile_total)
    slot_words = as_word_pair(my_slot)
    unit = row_width * chan_local
    word_rows = -(-slot_words.shape[0] // unit)
    slot_words = jnp.pad(slot_words, (0, word_rows * unit - slot_words.shape[0]))
    slot_words = slot_words.reshape(1, word_rows, row_width, chan_local)
    block_rows = jnp.moveaxis(returning, 0, 2).reshape(tile_total, capacity, row_width, chan_local)
    payload = jnp.concatenate(
        [block_rows, jnp.broadcast_to(slot_words, (tile_total, word_rows, row_width, chan_local))],
        axis=1,
    ).reshape(tile_total * (capacity + word_rows), row_width, chan_local)
    arrived_all = lax.all_to_all(payload, TILE, split_axis=0, concat_axis=0, tiled=True)
    arrived_all = arrived_all.reshape(tile_total, capacity + word_rows, row_width, chan_local)
    arrived = arrived_all[:, :capacity].reshape(tile_total * capacity, batch_rows, seg_len, chan_local)
    arrived = jnp.moveaxis(arrived, 1, 0)
    words = arrived_all[:, capacity:].reshape(tile_total, word_rows * row_width * chan_local)
    packed = from_word_pair(words[:, : 2 * my_slot.shape[0]]).reshape(-1)[: packed.shape[0]]
    block_ids = jnp.arange(block_total, dtype=jnp.int32)
    gather_back = (block_ids[:, None] == landing[None, :]).astype(jnp.bfloat16)
    summed = lax.dot_general(
        gather_back, arrived.reshape(tile_total * capacity, seg_len * chan_local),
        (((1,), (0,)), ((), ())), preferred_element_type=jnp.float32,
    )
    grad_latlon = summed.astype(jnp.bfloat16).reshape(batch_rows, block_total, seg_len, chan_local)
    kernel_sum = packed[: grad_kernel.size].reshape(grad_kernel.shape)
    mix_sum = packed[grad_kernel.size :].reshape(grad_mix.shape)
    if not exact_scale:
        kernel_sum = kernel_sum * factor
        mix_sum = mix_sum * factor
    return (coupled, grad_latlon, kernel_sum, mix_sum)


def physical_mesh(mesh):
    devices = mesh.devices
    tile_devs = devices[:, 0]
    x_count = len({d.coords[0] for d in tile_devs})
    y_count = len({d.coords[1] for d in tile_devs})
    zl_count = tile_devs.size // (x_count * y_count)
    zh_count = len({d.coords[2] for d in devices[0, :]})
    core_count = devices.shape[1] // zh_count
    shaped = devices.reshape(x_count, zl_count, y_count, zh_count, core_count)
    return Mesh(shaped, TILE + CHAN)


def solution(mesh):
    mesh = physical_mesh(mesh)
    return jax.shard_map(
        body,
        mesh=mesh,
        in_specs=(
            P(None, TILE, None, CHAN),
            P(TILE, None, None),
            P(),
            P(),
            P(),
            P(TILE),
            P(None, None, CHAN),
            P(),
            P(None, TILE, CHAN),
        ),
        out_specs=(
            P(None, TILE, CHAN),
            P(None, TILE, None, CHAN),
            P(None, None, CHAN),
            P(CHAN, None),
        ),
        check_vma=False,
    )
```

```python
import math

import jax
import jax.numpy as jnp
from jax import lax
from jax.sharding import Mesh, PartitionSpec as P

TILE_EDGE = 32
TILE = ("x", "zl", "y")
CHAN = ("zh", "core")


def turn_kernel(kernel, turn, direction):
    turned = jnp.zeros_like(kernel)
    for quarter in range(4):
        turned = turned + jnp.where(
            turn == quarter, jnp.rot90(kernel, direction * quarter, axes=(0, 1)), 0.0
        )
    return turned


def stencil_apply(field, kernel):
    shape_out = (field.shape[0], TILE_EDGE, TILE_EDGE, field.shape[3])
    hidden = jnp.zeros(shape_out, jnp.float32)
    for row_off in range(3):
        for col_off in range(3):
            window = field[
                :, row_off : row_off + TILE_EDGE, col_off : col_off + TILE_EDGE, :
            ].astype(jnp.float32)
            hidden = hidden + kernel[row_off, col_off] * window
    return hidden


def stencil_grads(field, kernel, grad_hidden):
    tap_rows = []
    grad_field = jnp.zeros(field.shape, jnp.float32)
    for row_off in range(3):
        tap_cols = []
        for col_off in range(3):
            window = field[
                :, row_off : row_off + TILE_EDGE, col_off : col_off + TILE_EDGE, :
            ].astype(jnp.float32)
            tap_cols.append(jnp.sum(window * grad_hidden, axis=(0, 1, 2)))
            spread = kernel[row_off, col_off] * grad_hidden
            grad_field = grad_field + jnp.pad(
                spread, ((0, 0), (row_off, 2 - row_off), (col_off, 2 - col_off), (0, 0))
            )
        tap_rows.append(jnp.stack(tap_cols))
    return (jnp.stack(tap_rows), grad_field)


def tile_partial(flat, parts):
    total = flat.shape[0]
    width = -(-total // (parts * 128)) * 128
    rows = jnp.pad(flat, (0, parts * width - total)).reshape(parts, width)
    pieces = lax.all_to_all(rows, TILE, split_axis=0, concat_axis=0, tiled=True)
    return jnp.sum(pieces, axis=0)


def as_word_pair(value):
    high = lax.reduce_precision(value, exponent_bits=8, mantissa_bits=7)
    low = value - high
    return jnp.concatenate([high.astype(jnp.bfloat16), low.astype(jnp.bfloat16)])


def from_word_pair(words):
    width = words.shape[-1] // 2
    return words[..., :width].astype(jnp.float32) + words[..., width:].astype(jnp.float32)


def body(
    latlon,
    remap_weights,
    term_source,
    term_block,
    term_count,
    rotation,
    depthwise,
    pointwise,
    cotangent,
):
    tile_now = lax.axis_index(TILE)
    tile_total = term_source.shape[0]
    chan_now = lax.axis_index(CHAN)
    batch_rows, block_total, seg_len, chan_local = latlon.shape
    terms_max = term_source.shape[1]
    capacity = 3 * terms_max // (2 * tile_total)
    ext_edge = TILE_EDGE + 2
    tile_cells = TILE_EDGE * TILE_EDGE
    flat_rows = batch_rows * tile_cells
    positions = jnp.arange(terms_max, dtype=jnp.int32)
    in_use = positions[None, :] < term_count[:, None]
    mine = in_use & (term_source == tile_now)
    send_rank = jnp.cumsum(mine.astype(jnp.int32), axis=1) - 1
    slot_ids = jnp.arange(capacity, dtype=jnp.int32)
    slot_hits = mine[:, :, None] & (send_rank[:, :, None] == slot_ids[None, None, :])
    slot_filled = jnp.any(slot_hits, axis=1).reshape(-1)
    slot_block = jnp.sum(jnp.where(slot_hits, term_block[:, :, None], 0), axis=1).reshape(-1)
    row_width = batch_rows * seg_len
    latlon_rows = jnp.moveaxis(latlon, 0, 1).reshape(block_total, row_width, chan_local)
    outgoing = jnp.take(latlon_rows, slot_block, axis=0, mode="clip")
    own_source = lax.dynamic_index_in_dim(term_source, tile_now, 0, keepdims=False)
    own_count = lax.dynamic_index_in_dim(term_count, tile_now, 0, keepdims=False)
    own_use = positions < own_count
    same_source = (
        (own_source[None, :] == own_source[:, None])
        & own_use[None, :]
        & (positions[None, :] <= positions[:, None])
    )
    own_rank = jnp.sum(same_source.astype(jnp.int32), axis=1) - 1
    recv_slot = jnp.where(own_use, own_source * capacity + own_rank, 0)
    return_slot = jnp.where(own_use, own_source * capacity + own_rank, tile_total * capacity)
    weights = remap_weights[0]
    ext_cells = weights.shape[0]
    term_pts = weights.shape[1]
    arrived = lax.all_to_all(outgoing, TILE, split_axis=0, concat_axis=0, tiled=True)
    picked = jnp.take(arrived, recv_slot, axis=0, mode="clip")
    picked = jnp.where(own_use[:, None, None], picked, jnp.zeros((), arrived.dtype))
    picked = picked.reshape(terms_max, batch_rows, seg_len, chan_local)
    picked = jnp.moveaxis(picked, 1, 0).reshape(batch_rows, term_pts, chan_local)
    mapped = jnp.einsum("pk,bkc->bpc", weights, picked, preferred_element_type=jnp.float32)
    remapped = mapped.astype(jnp.bfloat16)
    field = remapped.reshape(batch_rows, ext_edge, ext_edge, chan_local)
    turn = rotation[0]
    kernel = turn_kernel(depthwise.astype(jnp.float32), turn, 1)
    hidden = stencil_apply(field, kernel)
    active = jax.nn.silu(hidden).astype(jnp.bfloat16).reshape(flat_rows, chan_local)
    own_rows = lax.dynamic_slice_in_dim(pointwise, chan_now * chan_local, chan_local, 0)
    own_cols = lax.dynamic_slice_in_dim(pointwise, chan_now * chan_local, chan_local, 1)
    active_all = lax.all_gather(active, CHAN, axis=1, tiled=True)
    mixed = jnp.dot(active_all, own_cols, preferred_element_type=jnp.float32)
    coupled = mixed.astype(jnp.bfloat16).reshape(batch_rows, tile_cells, chan_local)
    upstream = cotangent.reshape(flat_rows, chan_local)
    piece = lax.all_gather(upstream, CHAN, axis=1, tiled=True)
    grad_active = lax.dot_general(
        piece, own_rows, (((1,), (1,)), ((), ())), preferred_element_type=jnp.float32
    )
    block_grad = lax.dot_general(
        active, piece, (((0,), (0,)), ((), ())), preferred_element_type=jnp.float32
    )
    grad_mix = block_grad
    grad_active, grad_mix = (grad_active, grad_mix)
    sigma = jax.nn.sigmoid(hidden)
    grad_hidden = grad_active.reshape(hidden.shape) * sigma * (1.0 + hidden * (1.0 - sigma))
    grad_turned, grad_field = stencil_grads(field, kernel, grad_hidden)
    grad_field = grad_field.astype(jnp.bfloat16).reshape(batch_rows, ext_cells, chan_local)
    grad_terms = jnp.einsum("pk,bpc->bkc", weights, grad_field, preferred_element_type=jnp.float32)
    grad_terms = grad_terms.reshape(batch_rows, terms_max, seg_len, chan_local)
    grad_terms = jnp.where(own_use[None, :, None, None], grad_terms, 0.0).astype(jnp.bfloat16)
    slot_all = jnp.arange(tile_total * capacity, dtype=jnp.int32)
    place = (slot_all[:, None] == return_slot[None, :]).astype(jnp.bfloat16)
    returning = jnp.einsum(
        "st,btc->bsc", place, grad_terms.reshape(batch_rows, terms_max, seg_len * chan_local),
        preferred_element_type=jnp.float32,
    ).astype(jnp.bfloat16).reshape(batch_rows, tile_total * capacity, seg_len, chan_local)
    landing = jnp.where(slot_filled, slot_block, block_total)
    grad_kernel = turn_kernel(grad_turned, turn, -1)
    factor = 1.0 / math.sqrt(batch_rows * tile_cells * tile_total)
    exact_scale = float(math.log2(factor)).is_integer()
    mix_rows, mix_cols = grad_mix.shape
    lane = 128
    sub = 8
    tiles = grad_mix.reshape(mix_rows // sub, sub, mix_cols // lane, lane).transpose(0, 2, 1, 3)
    tiles = tiles.reshape(-1, sub, lane)
    kernel_rows = grad_kernel.reshape(-1, lane)
    kernel_rows = jnp.pad(kernel_rows, ((0, tiles.shape[0] - kernel_rows.shape[0]), (0, 0)))
    slots = jnp.concatenate([tiles, kernel_rows[:, None, :]], axis=1)
    if exact_scale:
        slots = slots * factor
    my_slot = tile_partial(slots.reshape(-1), tile_total).reshape(sub + 1, lane)
    high = lax.reduce_precision(my_slot, exponent_bits=8, mantissa_bits=7)
    low = my_slot - high
    slot_words = jnp.concatenate(
        [high[:sub], low[:sub], high[sub:], low[sub:], jnp.zeros((sub - 2, lane), jnp.float32)], axis=0
    ).astype(jnp.bfloat16)
    word_rows = slot_words.shape[0] // sub
    slot_words = slot_words.reshape(1, word_rows, sub, lane)
    block_rows = jnp.moveaxis(returning, 0, 2).reshape(tile_total, capacity, row_width, chan_local)
    payload = jnp.concatenate(
        [block_rows, jnp.broadcast_to(slot_words, (tile_total, word_rows, row_width, chan_local))],
        axis=1,
    ).reshape(tile_total * (capacity + word_rows), row_width, chan_local)
    arrived_all = lax.all_to_all(payload, TILE, split_axis=0, concat_axis=0, tiled=True)
    arrived_all = arrived_all.reshape(tile_total, capacity + word_rows, row_width, chan_local)
    arrived = arrived_all[:, :capacity].reshape(tile_total * capacity, batch_rows, seg_len, chan_local)
    arrived = jnp.moveaxis(arrived, 1, 0)
    words = arrived_all[:, capacity:].reshape(tile_total, word_rows * sub, lane).astype(jnp.float32)
    mix_tiles = words[:, :sub] + words[:, sub : 2 * sub]
    kernel_part = words[:, 2 * sub] + words[:, 2 * sub + 1]
    mix_sum = mix_tiles.reshape(mix_rows // sub, mix_cols // lane, sub, lane).transpose(0, 2, 1, 3)
    mix_sum = mix_sum.reshape(mix_rows, mix_cols)
    kernel_sum = kernel_part[: grad_kernel.size // lane].reshape(grad_kernel.shape)
    block_ids = jnp.arange(block_total, dtype=jnp.int32)
    gather_back = (block_ids[:, None] == landing[None, :]).astype(jnp.bfloat16)
    summed = lax.dot_general(
        gather_back, arrived.reshape(tile_total * capacity, seg_len * chan_local),
        (((1,), (0,)), ((), ())), preferred_element_type=jnp.float32,
    )
    grad_latlon = summed.astype(jnp.bfloat16).reshape(batch_rows, block_total, seg_len, chan_local)
    if not exact_scale:
        kernel_sum = kernel_sum * factor
        mix_sum = mix_sum * factor
    return (coupled, grad_latlon, kernel_sum, mix_sum)


def physical_mesh(mesh):
    devices = mesh.devices
    tile_devs = devices[:, 0]
    x_count = len({d.coords[0] for d in tile_devs})
    y_count = len({d.coords[1] for d in tile_devs})
    zl_count = tile_devs.size // (x_count * y_count)
    zh_count = len({d.coords[2] for d in devices[0, :]})
    core_count = devices.shape[1] // zh_count
    shaped = devices.reshape(x_count, zl_count, y_count, zh_count, core_count)
    return Mesh(shaped, TILE + CHAN)


def solution(mesh):
    mesh = physical_mesh(mesh)
    return jax.shard_map(
        body,
        mesh=mesh,
        in_specs=(
            P(None, TILE, None, CHAN),
            P(TILE, None, None),
            P(),
            P(),
            P(),
            P(TILE),
            P(None, None, CHAN),
            P(),
            P(None, TILE, CHAN),
        ),
        out_specs=(
            P(None, TILE, CHAN),
            P(None, TILE, None, CHAN),
            P(None, None, CHAN),
            P(CHAN, None),
        ),
        check_vma=False,
    )
```

```python
import math

import jax
import jax.numpy as jnp
from jax import lax
from jax.sharding import Mesh, PartitionSpec as P

TILE_EDGE = 32
TILE = ("x", "zl", "y")
CHAN = ("zh", "core")


def turn_kernel(kernel, turn, direction):
    turned = jnp.zeros_like(kernel)
    for quarter in range(4):
        turned = turned + jnp.where(
            turn == quarter, jnp.rot90(kernel, direction * quarter, axes=(0, 1)), 0.0
        )
    return turned


def stencil_apply(field, kernel):
    shape_out = (field.shape[0], TILE_EDGE, TILE_EDGE, field.shape[3])
    hidden = jnp.zeros(shape_out, jnp.float32)
    for row_off in range(3):
        for col_off in range(3):
            window = field[
                :, row_off : row_off + TILE_EDGE, col_off : col_off + TILE_EDGE, :
            ].astype(jnp.float32)
            hidden = hidden + kernel[row_off, col_off] * window
    return hidden


def stencil_grads(field, kernel, grad_hidden):
    tap_rows = []
    grad_field = jnp.zeros(field.shape, jnp.float32)
    for row_off in range(3):
        tap_cols = []
        for col_off in range(3):
            window = field[
                :, row_off : row_off + TILE_EDGE, col_off : col_off + TILE_EDGE, :
            ].astype(jnp.float32)
            tap_cols.append(jnp.sum(window * grad_hidden, axis=(0, 1, 2)))
            spread = kernel[row_off, col_off] * grad_hidden
            grad_field = grad_field + jnp.pad(
                spread, ((0, 0), (row_off, 2 - row_off), (col_off, 2 - col_off), (0, 0))
            )
        tap_rows.append(jnp.stack(tap_cols))
    return (jnp.stack(tap_rows), grad_field)


def tile_partial(flat, parts):
    total = flat.shape[0]
    width = -(-total // (parts * 128)) * 128
    rows = jnp.pad(flat, (0, parts * width - total)).reshape(parts, width)
    pieces = lax.all_to_all(rows, TILE, split_axis=0, concat_axis=0, tiled=True)
    return jnp.sum(pieces, axis=0)


def body(
    latlon,
    remap_weights,
    term_source,
    term_block,
    term_count,
    rotation,
    depthwise,
    pointwise,
    cotangent,
):
    tile_now = lax.axis_index(TILE)
    tile_total = term_source.shape[0]
    chan_now = lax.axis_index(CHAN)
    batch_rows, block_total, seg_len, chan_local = latlon.shape
    terms_max = term_source.shape[1]
    capacity = 3 * terms_max // (2 * tile_total)
    ext_edge = TILE_EDGE + 2
    tile_cells = TILE_EDGE * TILE_EDGE
    flat_rows = batch_rows * tile_cells
    positions = jnp.arange(terms_max, dtype=jnp.int32)
    in_use = positions[None, :] < term_count[:, None]
    mine = in_use & (term_source == tile_now)
    send_rank = jnp.cumsum(mine.astype(jnp.int32), axis=1) - 1
    slot_ids = jnp.arange(capacity, dtype=jnp.int32)
    slot_hits = mine[:, :, None] & (send_rank[:, :, None] == slot_ids[None, None, :])
    slot_filled = jnp.any(slot_hits, axis=1).reshape(-1)
    slot_block = jnp.sum(jnp.where(slot_hits, term_block[:, :, None], 0), axis=1).reshape(-1)
    row_width = batch_rows * seg_len
    latlon_rows = jnp.moveaxis(latlon, 0, 1).reshape(block_total, row_width, chan_local)
    outgoing = jnp.take(latlon_rows, slot_block, axis=0, mode="clip")
    own_source = lax.dynamic_index_in_dim(term_source, tile_now, 0, keepdims=False)
    own_count = lax.dynamic_index_in_dim(term_count, tile_now, 0, keepdims=False)
    own_use = positions < own_count
    same_source = (
        (own_source[None, :] == own_source[:, None])
        & own_use[None, :]
        & (positions[None, :] <= positions[:, None])
    )
    own_rank = jnp.sum(same_source.astype(jnp.int32), axis=1) - 1
    recv_slot = jnp.where(own_use, own_source * capacity + own_rank, 0)
    return_slot = jnp.where(own_use, own_source * capacity + own_rank, tile_total * capacity)
    weights = remap_weights[0]
    ext_cells = weights.shape[0]
    term_pts = weights.shape[1]
    arrived = lax.all_to_all(outgoing, TILE, split_axis=0, concat_axis=0, tiled=True)
    picked = jnp.take(arrived, recv_slot, axis=0, mode="clip")
    picked = jnp.where(own_use[:, None, None], picked, jnp.zeros((), arrived.dtype))
    picked = picked.reshape(terms_max, batch_rows, seg_len, chan_local)
    picked = jnp.moveaxis(picked, 1, 0).reshape(batch_rows, term_pts, chan_local)
    mapped = jnp.einsum("pk,bkc->bpc", weights, picked, preferred_element_type=jnp.float32)
    remapped = mapped.astype(jnp.bfloat16)
    field = remapped.reshape(batch_rows, ext_edge, ext_edge, chan_local)
    turn = rotation[0]
    kernel = turn_kernel(depthwise.astype(jnp.float32), turn, 1)
    hidden = stencil_apply(field, kernel)
    active = jax.nn.silu(hidden).astype(jnp.bfloat16).reshape(flat_rows, chan_local)
    own_rows = lax.dynamic_slice_in_dim(pointwise, chan_now * chan_local, chan_local, 0)
    own_cols = lax.dynamic_slice_in_dim(pointwise, chan_now * chan_local, chan_local, 1)
    active_all = lax.all_gather(active, CHAN, axis=1, tiled=True)
    mixed = jnp.dot(active_all, own_cols, preferred_element_type=jnp.float32)
    coupled = mixed.astype(jnp.bfloat16).reshape(batch_rows, tile_cells, chan_local)
    upstream = cotangent.reshape(flat_rows, chan_local)
    piece = lax.all_gather(upstream, CHAN, axis=1, tiled=True)
    grad_active = lax.dot_general(
        piece, own_rows, (((1,), (1,)), ((), ())), preferred_element_type=jnp.float32
    )
    block_grad = lax.dot_general(
        active, piece, (((0,), (0,)), ((), ())), preferred_element_type=jnp.float32
    )
    grad_mix = block_grad
    grad_active, grad_mix = (grad_active, grad_mix)
    sigma = jax.nn.sigmoid(hidden)
    grad_hidden = grad_active.reshape(hidden.shape) * sigma * (1.0 + hidden * (1.0 - sigma))
    grad_turned, grad_field = stencil_grads(field, kernel, grad_hidden)
    grad_field = grad_field.astype(jnp.bfloat16).reshape(batch_rows, ext_cells, chan_local)
    grad_terms = jnp.einsum("pk,bpc->bkc", weights, grad_field, preferred_element_type=jnp.float32)
    grad_terms = grad_terms.reshape(batch_rows, terms_max, seg_len, chan_local)
    grad_terms = jnp.where(own_use[None, :, None, None], grad_terms, 0.0).astype(jnp.bfloat16)
    slot_all = jnp.arange(tile_total * capacity, dtype=jnp.int32)
    place = (slot_all[:, None] == return_slot[None, :]).astype(jnp.bfloat16)
    returning = jnp.einsum(
        "st,btc->bsc", place, grad_terms.reshape(batch_rows, terms_max, seg_len * chan_local),
        preferred_element_type=jnp.float32,
    ).astype(jnp.bfloat16).reshape(batch_rows, tile_total * capacity, seg_len, chan_local)
    landing = jnp.where(slot_filled, slot_block, block_total)
    grad_kernel = turn_kernel(grad_turned, turn, -1)
    packed = jnp.concatenate([grad_kernel.reshape(-1), grad_mix.reshape(-1)])
    factor = 1.0 / math.sqrt(batch_rows * tile_cells * tile_total)
    exact_scale = float(math.log2(factor)).is_integer()
    if exact_scale:
        packed = packed * factor
    my_slot = tile_partial(packed, tile_total)
    slot_words = my_slot.astype(jnp.bfloat16)
    unit = row_width * chan_local
    word_rows = -(-slot_words.shape[0] // unit)
    slot_words = jnp.pad(slot_words, (0, word_rows * unit - slot_words.shape[0]))
    slot_words = slot_words.reshape(1, word_rows, row_width, chan_local)
    block_rows = jnp.moveaxis(returning, 0, 2).reshape(tile_total, capacity, row_width, chan_local)
    payload = jnp.concatenate(
        [block_rows, jnp.broadcast_to(slot_words, (tile_total, word_rows, row_width, chan_local))],
        axis=1,
    ).reshape(tile_total * (capacity + word_rows), row_width, chan_local)
    arrived_all = lax.all_to_all(payload, TILE, split_axis=0, concat_axis=0, tiled=True)
    arrived_all = arrived_all.reshape(tile_total, capacity + word_rows, row_width, chan_local)
    arrived = arrived_all[:, :capacity].reshape(tile_total * capacity, batch_rows, seg_len, chan_local)
    arrived = jnp.moveaxis(arrived, 1, 0)
    words = arrived_all[:, capacity:].reshape(tile_total, word_rows * row_width * chan_local)
    packed = words[:, : my_slot.shape[0]].astype(jnp.float32).reshape(-1)[: packed.shape[0]]
    block_ids = jnp.arange(block_total, dtype=jnp.int32)
    gather_back = (block_ids[:, None] == landing[None, :]).astype(jnp.bfloat16)
    summed = lax.dot_general(
        gather_back, arrived.reshape(tile_total * capacity, seg_len * chan_local),
        (((1,), (0,)), ((), ())), preferred_element_type=jnp.float32,
    )
    grad_latlon = summed.astype(jnp.bfloat16).reshape(batch_rows, block_total, seg_len, chan_local)
    kernel_sum = packed[: grad_kernel.size].reshape(grad_kernel.shape)
    mix_sum = packed[grad_kernel.size :].reshape(grad_mix.shape)
    if not exact_scale:
        kernel_sum = kernel_sum * factor
        mix_sum = mix_sum * factor
    return (coupled, grad_latlon, kernel_sum, mix_sum)


def physical_mesh(mesh):
    devices = mesh.devices
    tile_devs = devices[:, 0]
    x_count = len({d.coords[0] for d in tile_devs})
    y_count = len({d.coords[1] for d in tile_devs})
    zl_count = tile_devs.size // (x_count * y_count)
    zh_count = len({d.coords[2] for d in devices[0, :]})
    core_count = devices.shape[1] // zh_count
    shaped = devices.reshape(x_count, zl_count, y_count, zh_count, core_count)
    return Mesh(shaped, TILE + CHAN)


def solution(mesh):
    mesh = physical_mesh(mesh)
    return jax.shard_map(
        body,
        mesh=mesh,
        in_specs=(
            P(None, TILE, None, CHAN),
            P(TILE, None, None),
            P(),
            P(),
            P(),
            P(TILE),
            P(None, None, CHAN),
            P(),
            P(None, TILE, CHAN),
        ),
        out_specs=(
            P(None, TILE, CHAN),
            P(None, TILE, None, CHAN),
            P(None, None, CHAN),
            P(CHAN, None),
        ),
        check_vma=False,
    )
```

```python
import math

import jax
import jax.numpy as jnp
from jax import lax
from jax.sharding import Mesh, PartitionSpec as P

TILE_EDGE = 32
TILE = ("x", "zl", "y")
CHAN = ("zh", "core")


def turn_kernel(kernel, turn, direction):
    turned = jnp.zeros_like(kernel)
    for quarter in range(4):
        turned = turned + jnp.where(
            turn == quarter, jnp.rot90(kernel, direction * quarter, axes=(0, 1)), 0.0
        )
    return turned


def stencil_apply(field, kernel):
    shape_out = (field.shape[0], TILE_EDGE, TILE_EDGE, field.shape[3])
    hidden = jnp.zeros(shape_out, jnp.float32)
    for row_off in range(3):
        for col_off in range(3):
            window = field[
                :, row_off : row_off + TILE_EDGE, col_off : col_off + TILE_EDGE, :
            ].astype(jnp.float32)
            hidden = hidden + kernel[row_off, col_off] * window
    return hidden


def stencil_grads(field, kernel, grad_hidden):
    tap_rows = []
    grad_field = jnp.zeros(field.shape, jnp.float32)
    for row_off in range(3):
        tap_cols = []
        for col_off in range(3):
            window = field[
                :, row_off : row_off + TILE_EDGE, col_off : col_off + TILE_EDGE, :
            ].astype(jnp.float32)
            tap_cols.append(jnp.sum(window * grad_hidden, axis=(0, 1, 2)))
            spread = kernel[row_off, col_off] * grad_hidden
            grad_field = grad_field + jnp.pad(
                spread, ((0, 0), (row_off, 2 - row_off), (col_off, 2 - col_off), (0, 0))
            )
        tap_rows.append(jnp.stack(tap_cols))
    return (jnp.stack(tap_rows), grad_field)


def tile_partial(flat, parts):
    total = flat.shape[0]
    width = -(-total // (parts * 128)) * 128
    rows = jnp.pad(flat, (0, parts * width - total)).reshape(parts, width)
    pieces = lax.all_to_all(rows, TILE, split_axis=0, concat_axis=0, tiled=True)
    return jnp.sum(pieces, axis=0)


def body(
    latlon,
    remap_weights,
    term_source,
    term_block,
    term_count,
    rotation,
    depthwise,
    pointwise,
    cotangent,
):
    tile_now = lax.axis_index(TILE)
    tile_total = term_source.shape[0]
    chan_now = lax.axis_index(CHAN)
    batch_rows, block_total, seg_len, chan_local = latlon.shape
    terms_max = term_source.shape[1]
    capacity = 3 * terms_max // (2 * tile_total)
    ext_edge = TILE_EDGE + 2
    tile_cells = TILE_EDGE * TILE_EDGE
    flat_rows = batch_rows * tile_cells
    positions = jnp.arange(terms_max, dtype=jnp.int32)
    in_use = positions[None, :] < term_count[:, None]
    mine = in_use & (term_source == tile_now)
    send_rank = jnp.cumsum(mine.astype(jnp.int32), axis=1) - 1
    slot_ids = jnp.arange(capacity, dtype=jnp.int32)
    slot_hits = mine[:, :, None] & (send_rank[:, :, None] == slot_ids[None, None, :])
    slot_filled = jnp.any(slot_hits, axis=1).reshape(-1)
    slot_block = jnp.sum(jnp.where(slot_hits, term_block[:, :, None], 0), axis=1).reshape(-1)
    row_width = batch_rows * seg_len
    latlon_rows = jnp.moveaxis(latlon, 0, 1).reshape(block_total, row_width, chan_local)
    outgoing = jnp.take(latlon_rows, slot_block, axis=0, mode="clip")
    own_source = lax.dynamic_index_in_dim(term_source, tile_now, 0, keepdims=False)
    own_count = lax.dynamic_index_in_dim(term_count, tile_now, 0, keepdims=False)
    own_use = positions < own_count
    same_source = (
        (own_source[None, :] == own_source[:, None])
        & own_use[None, :]
        & (positions[None, :] <= positions[:, None])
    )
    own_rank = jnp.sum(same_source.astype(jnp.int32), axis=1) - 1
    recv_slot = jnp.where(own_use, own_source * capacity + own_rank, 0)
    return_slot = jnp.where(own_use, own_source * capacity + own_rank, tile_total * capacity)
    weights = remap_weights[0]
    ext_cells = weights.shape[0]
    term_pts = weights.shape[1]
    arrived = lax.all_to_all(outgoing, TILE, split_axis=0, concat_axis=0, tiled=True)
    picked = jnp.take(arrived, recv_slot, axis=0, mode="clip")
    picked = jnp.where(own_use[:, None, None], picked, jnp.zeros((), arrived.dtype))
    picked = picked.reshape(terms_max, batch_rows, seg_len, chan_local)
    picked = jnp.moveaxis(picked, 1, 0).reshape(batch_rows, term_pts, chan_local)
    mapped = jnp.einsum("pk,bkc->bpc", weights, picked, preferred_element_type=jnp.float32)
    remapped = mapped.astype(jnp.bfloat16)
    field = remapped.reshape(batch_rows, ext_edge, ext_edge, chan_local)
    turn = rotation[0]
    kernel = turn_kernel(depthwise.astype(jnp.float32), turn, 1)
    hidden = stencil_apply(field, kernel)
    active = jax.nn.silu(hidden).astype(jnp.bfloat16).reshape(flat_rows, chan_local)
    own_rows = lax.dynamic_slice_in_dim(pointwise, chan_now * chan_local, chan_local, 0)
    own_cols = lax.dynamic_slice_in_dim(pointwise, chan_now * chan_local, chan_local, 1)
    active_all = lax.all_gather(active, CHAN, axis=1, tiled=True)
    mixed = jnp.dot(active_all, own_cols, preferred_element_type=jnp.float32)
    coupled = mixed.astype(jnp.bfloat16).reshape(batch_rows, tile_cells, chan_local)
    upstream = cotangent.reshape(flat_rows, chan_local)
    piece = lax.all_gather(upstream, CHAN, axis=1, tiled=True)
    grad_active = lax.dot_general(
        piece, own_rows, (((1,), (1,)), ((), ())), preferred_element_type=jnp.float32
    )
    block_grad = lax.dot_general(
        active, piece, (((0,), (0,)), ((), ())), preferred_element_type=jnp.float32
    )
    grad_mix = block_grad
    grad_active, grad_mix = (grad_active, grad_mix)
    sigma = jax.nn.sigmoid(hidden)
    grad_hidden = grad_active.reshape(hidden.shape) * sigma * (1.0 + hidden * (1.0 - sigma))
    grad_turned, grad_field = stencil_grads(field, kernel, grad_hidden)
    grad_field = grad_field.astype(jnp.bfloat16).reshape(batch_rows, ext_cells, chan_local)
    grad_terms = jnp.einsum("pk,bpc->bkc", weights, grad_field, preferred_element_type=jnp.float32)
    grad_terms = grad_terms.reshape(batch_rows, terms_max, seg_len, chan_local)
    grad_terms = jnp.where(own_use[None, :, None, None], grad_terms, 0.0).astype(jnp.bfloat16)
    slot_all = jnp.arange(tile_total * capacity, dtype=jnp.int32)
    place = (slot_all[:, None] == return_slot[None, :]).astype(jnp.bfloat16)
    returning = jnp.einsum(
        "st,btc->bsc", place, grad_terms.reshape(batch_rows, terms_max, seg_len * chan_local),
        preferred_element_type=jnp.float32,
    ).astype(jnp.bfloat16).reshape(batch_rows, tile_total * capacity, seg_len, chan_local)
    landing = jnp.where(slot_filled, slot_block, block_total)
    grad_kernel = turn_kernel(grad_turned, turn, -1)
    packed = jnp.concatenate([grad_kernel.reshape(-1), grad_mix.reshape(-1)])
    factor = 1.0 / math.sqrt(batch_rows * tile_cells * tile_total)
    exact_scale = float(math.log2(factor)).is_integer()
    if exact_scale:
        packed = packed * factor
    my_slot = tile_partial(packed, tile_total)
    slot_words = my_slot.astype(jnp.bfloat16)
    unit = row_width * chan_local
    word_rows = -(-slot_words.shape[0] // unit)
    slot_words = jnp.pad(slot_words, (0, word_rows * unit - slot_words.shape[0]))
    slot_words = slot_words.reshape(1, word_rows, row_width, chan_local)
    block_rows = jnp.moveaxis(returning, 0, 2).reshape(tile_total, capacity, row_width, chan_local)
    payload = lax.optimization_barrier(jnp.pad(block_rows, ((0, 0), (0, word_rows), (0, 0), (0, 0))))
    payload = payload.at[:, capacity:].set(
        jnp.broadcast_to(slot_words, (tile_total, word_rows, row_width, chan_local))
    ).reshape(tile_total * (capacity + word_rows), row_width, chan_local)
    arrived_all = lax.all_to_all(payload, TILE, split_axis=0, concat_axis=0, tiled=True)
    arrived_all = arrived_all.reshape(tile_total, capacity + word_rows, row_width, chan_local)
    arrived = arrived_all[:, :capacity].reshape(tile_total * capacity, batch_rows, seg_len, chan_local)
    arrived = jnp.moveaxis(arrived, 1, 0)
    words = arrived_all[:, capacity:].reshape(tile_total, word_rows * row_width * chan_local)
    packed = words[:, : my_slot.shape[0]].astype(jnp.float32).reshape(-1)[: packed.shape[0]]
    block_ids = jnp.arange(block_total, dtype=jnp.int32)
    gather_back = (block_ids[:, None] == landing[None, :]).astype(jnp.bfloat16)
    summed = lax.dot_general(
        gather_back, arrived.reshape(tile_total * capacity, seg_len * chan_local),
        (((1,), (0,)), ((), ())), preferred_element_type=jnp.float32,
    )
    grad_latlon = summed.astype(jnp.bfloat16).reshape(batch_rows, block_total, seg_len, chan_local)
    kernel_sum = packed[: grad_kernel.size].reshape(grad_kernel.shape)
    mix_sum = packed[grad_kernel.size :].reshape(grad_mix.shape)
    if not exact_scale:
        kernel_sum = kernel_sum * factor
        mix_sum = mix_sum * factor
    return (coupled, grad_latlon, kernel_sum, mix_sum)


def physical_mesh(mesh):
    devices = mesh.devices
    tile_devs = devices[:, 0]
    x_count = len({d.coords[0] for d in tile_devs})
    y_count = len({d.coords[1] for d in tile_devs})
    zl_count = tile_devs.size // (x_count * y_count)
    zh_count = len({d.coords[2] for d in devices[0, :]})
    core_count = devices.shape[1] // zh_count
    shaped = devices.reshape(x_count, zl_count, y_count, zh_count, core_count)
    return Mesh(shaped, TILE + CHAN)


def solution(mesh):
    mesh = physical_mesh(mesh)
    return jax.shard_map(
        body,
        mesh=mesh,
        in_specs=(
            P(None, TILE, None, CHAN),
            P(TILE, None, None),
            P(),
            P(),
            P(),
            P(TILE),
            P(None, None, CHAN),
            P(),
            P(None, TILE, CHAN),
        ),
        out_specs=(
            P(None, TILE, CHAN),
            P(None, TILE, None, CHAN),
            P(None, None, CHAN),
            P(CHAN, None),
        ),
        check_vma=False,
    )
```
